32 devices in a mesh: blk: 8 (over z, y), corpus: 4 (over x, core).
Axes of the slice: x: 2, y: 2, z: 4, core: 2. Of those that a mesh axis runs over, the one named last changes fastest.
Arguments:
- queries: bfloat16 [1024, 4096], P('blk', 'corpus'), may hold values from -12 to 12
- passages: bfloat16 [1024, 4096], P('blk', 'corpus'), may hold values from -4 to 4
- table: bfloat16 [1024, 4096], P('corpus'), may hold values from -4 to 4
- neg_owner: int32 [1024, 7], P('blk'), may hold values from 0 to 3, as said below
- neg_row: int32 [1024, 7], P('blk'), may hold values from 0 to 255
- positive: int32 [1024], P('blk'), may hold values from 0 to 1023, each once
- loss_weight: float32 [1024], P('blk'), may hold values from 32 to 256
Outputs:
- losses: float32 [1024], P(('blk', 'corpus'))
- query_grad: float32 [1024, 4096], P('blk', 'corpus')
- passage_grad: float32 [1024, 4096], P('blk', 'corpus')
- table_grad: float32 [1024, 4096], P('corpus', 'blk')
The draws below stay inside these ranges and needn't reach their ends.
Inputs may be any that keep to these rules, and one draw needn't show every extreme that they name: `neg_owner`: among the 896 references of the queries of one index of blk (aligned blocks of 128 queries), one shard is named exactly 448 times and no shard more often.
All inputs are finite; a program needn't handle non-finite values.
Results may differ from the reference program's by a relative error of at most 0.0065.
Values may be sent and summed in bfloat16 or wider, within the bound.
No kernel may reach another device: no remote copies, remote signals or barrier semaphores. Data moves between devices by JAX's collectives and lax.ppermute only.
A program may use at most 128 MiB of HBM per device.

```python
import math
import jax
import jax.numpy as jnp

D = 4096
Q_BLK = 128
NEGS = 7
ROWS_SH = 256
B = 1024
CAP = 448
CROWS = 1024
N_CORPUS = 4


def common_draw(key):
    block_refs = Q_BLK * NEGS
    blocks = B // Q_BLK
    hot_owner = jax.random.randint(jax.random.fold_in(key, 11), (blocks, 1), 0, N_CORPUS)
    offsets = jax.random.randint(jax.random.fold_in(key, 12), (blocks, block_refs), 1, N_CORPUS)
    places = jnp.arange(block_refs)[None, :]
    ordered = jnp.where(places < CAP, hot_owner, (hot_owner + offsets) % N_CORPUS)
    block_keys = jax.random.split(jax.random.fold_in(key, 13), blocks)
    orders = jax.vmap(lambda sub_key: jax.random.permutation(sub_key, block_refs))(block_keys)
    owners = jnp.take_along_axis(ordered, orders, axis=1).reshape(B, NEGS).astype(jnp.int32)
    shard_rows = jax.random.randint(jax.random.fold_in(key, 14), (B, NEGS), 0, ROWS_SH).astype(jnp.int32)
    table = jnp.clip(jax.random.normal(jax.random.fold_in(key, 15), (CROWS, D)), -4.0, 4.0)
    passages = jnp.clip(jax.random.normal(jax.random.fold_in(key, 16), (B, D)), -4.0, 4.0)
    noise = jnp.clip(jax.random.normal(jax.random.fold_in(key, 18), (B, D)), -4.0, 4.0)
    table_ids = owners * ROWS_SH + shard_rows
    hard_sum = jnp.zeros((B, D), jnp.float32)
    for which in range(NEGS):
        hard_sum = hard_sum + table[table_ids[:, which]]
    queries = noise + 0.07 * hard_sum
    return (owners, shard_rows, table, passages, queries)


def draw_queries(key, part):
    return common_draw(key)[4].astype(jnp.bfloat16)


def draw_passages(key, part):
    return common_draw(key)[3].astype(jnp.bfloat16)


def draw_table(key, part):
    return common_draw(key)[2].astype(jnp.bfloat16)


def draw_neg_owner(key, part):
    return common_draw(key)[0]


def draw_neg_row(key, part):
    return common_draw(key)[1]


def shard_levels(stream_key, dims, cuts, least, largest):
    gain, own = 1.0, jax.random.fold_in(stream_key, 6)
    for dim, parts in cuts:
        steps = jnp.exp(jax.random.uniform(jax.random.fold_in(own, dim), (parts,), jnp.float32, least / len(cuts), largest / len(cuts)))
        gain = gain * jnp.repeat(steps, dims[dim] // parts).reshape([-1 if axis == dim else 1 for axis in range(len(dims))])
    return gain


def setup_inputs(seed: int = 0) -> dict:
    keys = jax.random.split(jax.random.key(seed), 8)
    queries = draw_queries(jax.random.fold_in(keys[7], 71), 0)
    passages = draw_passages(jax.random.fold_in(keys[7], 71), 0)
    table = draw_table(jax.random.fold_in(keys[7], 71), 0)
    neg_owner = draw_neg_owner(jax.random.fold_in(keys[7], 71), 0)
    neg_row = draw_neg_row(jax.random.fold_in(keys[7], 71), 0)
    positive = jax.random.permutation(keys[5], B).astype(jnp.int32)
    loss_weight = jnp.clip(jnp.exp(math.log(256.0) - 2.0794415 * jax.random.uniform(keys[6], (B,), jnp.float32) ** shard_levels(keys[6], (B,), ((0, 8),), -0.2, 0.2)), 32.0, 256.0)
    return {"queries": queries, "passages": passages, "table": table, "neg_owner": neg_owner, "neg_row": neg_row, "positive": positive, "loss_weight": loss_weight}


def reference(queries, passages, table, neg_owner, neg_row, positive, loss_weight):
    factor = queries.shape[1] ** -0.5
    table_ids = (neg_owner * ROWS_SH + neg_row).astype(jnp.int32)
    logits = jnp.dot(queries, passages.T, preferred_element_type=jnp.float32) * factor
    query_wide = queries.astype(jnp.float32)
    gathered = []
    hard_cols = []
    for which in range(NEGS):
        neg_rows = table[table_ids[:, which]].astype(jnp.float32)
        gathered.append(neg_rows)
        hard_cols.append(jnp.sum(query_wide * neg_rows, axis=1) * factor)
    hard_logits = jnp.stack(hard_cols, axis=1)
    row_top = jnp.maximum(jnp.max(logits, axis=1), jnp.max(hard_logits, axis=1))
    log_total = row_top + jnp.log(jnp.sum(jnp.exp(logits - row_top[:, None]), axis=1) + jnp.sum(jnp.exp(hard_logits - row_top[:, None]), axis=1))
    one_hot = positive[:, None] == jnp.arange(logits.shape[1], dtype=jnp.int32)[None, :]
    losses = log_total - jnp.sum(jnp.where(one_hot, logits, jnp.float32(0.0)), axis=1)
    weighting = (loss_weight * factor)[:, None]
    soft_grad = (weighting * (jnp.exp(logits - log_total[:, None]) - one_hot.astype(jnp.float32))).astype(jnp.bfloat16)
    hard_grad = (weighting * jnp.exp(hard_logits - log_total[:, None])).astype(jnp.bfloat16)
    query_grad = jnp.dot(soft_grad, passages, preferred_element_type=jnp.float32)
    table_grad = jnp.zeros((table.shape[0], table.shape[1]), jnp.float32)
    for which in range(NEGS):
        column_grad = hard_grad[:, which:which + 1].astype(jnp.float32)
        query_grad = query_grad + column_grad * gathered[which]
        table_grad = table_grad.at[table_ids[:, which]].add(column_grad * query_wide)
    passage_grad = jnp.dot(soft_grad.T, queries, preferred_element_type=jnp.float32)
    return losses, query_grad, passage_grad, table_grad
```

```python
import jax
import jax.numpy as jnp
from jax import lax
from jax.sharding import PartitionSpec as P


def hi_lo(mixing):
    upper = mixing.astype(jnp.bfloat16)
    lower = (mixing - upper.astype(jnp.float32)).astype(jnp.bfloat16)
    return upper, lower


def per_device(queries, passages, table, neg_owner, neg_row, positive, loss_weight):
    q_rows, col_width = queries.shape
    owner_count = lax.axis_size("corpus")
    blk_count = lax.axis_size("blk")
    factor = (col_width * owner_count) ** (-0.5)
    rows_shard = table.shape[0]
    table_rows = owner_count * rows_shard
    owner_index = lax.axis_index("corpus")
    blk_index = lax.axis_index("blk")

    table_cols = lax.all_to_all(table, "corpus", split_axis=1, concat_axis=0, tiled=True)
    all_passages = lax.all_gather(passages, "blk", axis=0, tiled=True)
    all_queries = lax.all_gather(queries, "blk", axis=0, tiled=True)
    ids = neg_owner * rows_shard + neg_row
    all_ids = lax.all_gather(ids, "blk", axis=0, tiled=True)
    all_rows = all_passages.shape[0]

    logits = lax.dot_general(
        queries, all_passages, (((1,), (1,)), ((), ())), preferred_element_type=jnp.float32
    )
    table_scores = lax.dot_general(
        queries, table_cols, (((1,), (1,)), ((), ())), preferred_element_type=jnp.float32
    )
    row_iota = jnp.arange(table_rows, dtype=jnp.int32)
    picks = ids[:, :, None] == row_iota[None, None, :]
    hard_logits = jnp.sum(jnp.where(picks, table_scores[:, None, :], 0.0), axis=2)
    logits, hard_logits = lax.psum((logits, hard_logits), "corpus")
    logits = logits * factor
    hard_logits = hard_logits * factor
    row_top = jnp.maximum(jnp.max(logits, axis=1), jnp.max(hard_logits, axis=1))
    log_total = row_top + jnp.log(
        jnp.sum(jnp.exp(logits - row_top[:, None]), axis=1)
        + jnp.sum(jnp.exp(hard_logits - row_top[:, None]), axis=1)
    )
    one_hot = positive[:, None] == jnp.arange(all_rows, dtype=jnp.int32)[None, :]
    losses = log_total - jnp.sum(jnp.where(one_hot, logits, 0.0), axis=1)
    share = q_rows // owner_count
    loss_share = lax.dynamic_slice_in_dim(losses, owner_index * share, share)
    weighting = (loss_weight * factor)[:, None]
    soft_grad = (
        weighting * (jnp.exp(logits - log_total[:, None]) - one_hot.astype(jnp.float32))
    ).astype(jnp.bfloat16)
    hard_grad = (weighting * jnp.exp(hard_logits - log_total[:, None])).astype(jnp.bfloat16)

    mixing = jnp.sum(jnp.where(picks, hard_grad.astype(jnp.float32)[:, :, None], 0.0), axis=1)
    mix_hi, mix_lo = hi_lo(mixing)
    left = jnp.concatenate([soft_grad, mix_hi, mix_lo], axis=1)
    right = jnp.concatenate([all_passages, table_cols, table_cols], axis=0)
    query_grad = jnp.dot(left, right, preferred_element_type=jnp.float32)

    soft_cols = lax.all_to_all(soft_grad, "blk", split_axis=1, concat_axis=0, tiled=True)
    passage_grad = lax.dot_general(
        soft_cols, all_queries, (((0,), (0,)), ((), ())), preferred_element_type=jnp.float32
    )

    all_hard = lax.all_gather(hard_grad, "blk", axis=0, tiled=True)
    per_col = blk_count // owner_count
    piece_width = col_width // per_col
    shard = blk_index // per_col
    part = blk_index % per_col
    shard_iota = shard * rows_shard + jnp.arange(rows_shard, dtype=jnp.int32)
    shard_picks = all_ids[:, :, None] == shard_iota[None, None, :]
    shard_mix = jnp.sum(
        jnp.where(shard_picks, all_hard.astype(jnp.float32)[:, :, None], 0.0), axis=1
    )
    shard_hi, shard_lo = hi_lo(shard_mix)
    query_part = lax.dynamic_slice_in_dim(all_queries, part * piece_width, piece_width, axis=1)
    dims = (((0,), (0,)), ((), ()))
    piece = lax.dot_general(
        shard_hi, query_part, dims, preferred_element_type=jnp.float32
    ) + lax.dot_general(shard_lo, query_part, dims, preferred_element_type=jnp.float32)
    perm = []
    for b in range(blk_count):
        for c in range(owner_count):
            dest_b = c * per_col + b % per_col
            dest_c = b // per_col
            perm.append((b * owner_count + c, dest_b * owner_count + dest_c))
    table_grad = lax.ppermute(piece, ("blk", "corpus"), perm)
    return (loss_share, query_grad, passage_grad, table_grad)


def solution(mesh):
    placed = (
        P("blk", "corpus"),
        P("blk", "corpus"),
        P("corpus", None),
        P("blk", None),
        P("blk", None),
        P("blk"),
        P("blk"),
    )
    return jax.shard_map(
        per_device,
        mesh=mesh,
        in_specs=placed,
        out_specs=(
            P(("blk", "corpus")),
            P("blk", "corpus"),
            P("blk", "corpus"),
            P("corpus", "blk"),
        ),
        check_vma=False,
    )
```

```python
import jax
import jax.numpy as jnp
from jax import lax
from jax.sharding import PartitionSpec as P


def hi_lo(mixing):
    upper = mixing.astype(jnp.bfloat16)
    lower = (mixing - upper.astype(jnp.float32)).astype(jnp.bfloat16)
    return upper, lower


def per_device_body(queries, passages, table, neg_owner, neg_row, positive, loss_weight):
    q_rows, col_width = queries.shape
    owner_count = lax.axis_size("corpus")
    blk_count = lax.axis_size("blk")
    factor = (col_width * owner_count) ** (-0.5)
    rows_shard = table.shape[0]
    table_rows = owner_count * rows_shard
    owner_index = lax.axis_index("corpus")
    blk_index = lax.axis_index("blk")

    slice_of = lambda k: lax.dynamic_slice_in_dim(
        table, ((owner_index + k) % owner_count) * col_width, col_width, axis=1
    )
    table_cols = jnp.zeros((table_rows, col_width), table.dtype)
    table_cols = lax.dynamic_update_slice_in_dim(
        table_cols, slice_of(0), owner_index * rows_shard, axis=0
    )
    for k in range(1, owner_count):
        shift = [(j, (j + k) % owner_count) for j in range(owner_count)]
        got = lax.ppermute(slice_of(k), "corpus", shift)
        source = (owner_index - k) % owner_count
        table_cols = lax.dynamic_update_slice_in_dim(table_cols, got, source * rows_shard, axis=0)
    all_passages = lax.all_gather(passages, "blk", axis=0, tiled=True)
    all_passages, later = lax.optimization_barrier((all_passages, queries))
    all_queries = jnp.zeros((blk_count * q_rows, col_width), queries.dtype)
    all_queries = lax.dynamic_update_slice_in_dim(all_queries, queries, blk_index * q_rows, axis=0)
    for k in range(1, blk_count):
        shift = [(j, (j + k) % blk_count) for j in range(blk_count)]
        got = lax.ppermute(later, "blk", shift)
        source = (blk_index - k) % blk_count
        all_queries = lax.dynamic_update_slice_in_dim(all_queries, got, source * q_rows, axis=0)
    ids = neg_owner * rows_shard + neg_row
    all_rows = all_passages.shape[0]

    logits = lax.dot_general(
        queries, all_passages, (((1,), (1,)), ((), ())), preferred_element_type=jnp.float32
    )
    table_scores = lax.dot_general(
        queries, table_cols, (((1,), (1,)), ((), ())), preferred_element_type=jnp.float32
    )
    row_iota = jnp.arange(table_rows, dtype=jnp.int32)
    picks = ids[:, :, None] == row_iota[None, None, :]
    hard_logits = jnp.sum(jnp.where(picks, table_scores[:, None, :], 0.0), axis=2)
    negs = ids.shape[1]
    pad = jnp.zeros((q_rows, 128 - negs), jnp.float32)
    partial = jnp.concatenate([logits, hard_logits, pad], axis=1)
    share = q_rows // owner_count
    chunk_of = lambda k: lax.dynamic_slice_in_dim(
        partial, ((owner_index + k) % owner_count) * share, share, axis=0
    )
    summed = chunk_of(0)
    for k in range(1, owner_count):
        shift = [(j, (j + k) % owner_count) for j in range(owner_count)]
        got = lax.ppermute(chunk_of(k), "corpus", shift)
        summed = summed + got
    logits = summed[:, :all_rows] * factor
    hard_logits = summed[:, all_rows:all_rows + negs] * factor
    my_positive = lax.dynamic_slice_in_dim(positive, owner_index * share, share)
    my_weight = lax.dynamic_slice_in_dim(loss_weight, owner_index * share, share)
    row_top = jnp.maximum(jnp.max(logits, axis=1), jnp.max(hard_logits, axis=1))
    log_total = row_top + jnp.log(
        jnp.sum(jnp.exp(logits - row_top[:, None]), axis=1)
        + jnp.sum(jnp.exp(hard_logits - row_top[:, None]), axis=1)
    )
    one_hot = my_positive[:, None] == jnp.arange(all_rows, dtype=jnp.int32)[None, :]
    loss_share = log_total - jnp.sum(jnp.where(one_hot, logits, 0.0), axis=1)
    weighting = (my_weight * factor)[:, None]
    soft_part = (
        weighting * (jnp.exp(logits - log_total[:, None]) - one_hot.astype(jnp.float32))
    ).astype(jnp.bfloat16)
    hard_part = (weighting * jnp.exp(hard_logits - log_total[:, None])).astype(jnp.bfloat16)
    grads_part = jnp.concatenate(
        [soft_part, hard_part, jnp.zeros((share, 128 - negs), jnp.bfloat16)], axis=1
    )
    grads = jnp.zeros((q_rows, grads_part.shape[1]), jnp.bfloat16)
    grads = lax.dynamic_update_slice_in_dim(grads, grads_part, owner_index * share, axis=0)
    for k in range(1, owner_count):
        shift = [(j, (j + k) % owner_count) for j in range(owner_count)]
        got = lax.ppermute(grads_part, "corpus", shift)
        source = (owner_index - k) % owner_count
        grads = lax.dynamic_update_slice_in_dim(grads, got, source * share, axis=0)
    soft_grad = grads[:, :all_rows]
    hard_grad = grads[:, all_rows:all_rows + negs]

    mixing = jnp.sum(jnp.where(picks, hard_grad.astype(jnp.float32)[:, :, None], 0.0), axis=1)
    mix_hi, mix_lo = hi_lo(mixing)
    left = jnp.concatenate([soft_grad, mix_hi, mix_lo], axis=1)
    right = jnp.concatenate([all_passages, table_cols, table_cols], axis=0)
    query_grad = jnp.dot(left, right, preferred_element_type=jnp.float32)

    extra = jnp.concatenate(
        [
            hard_grad,
            neg_owner.astype(jnp.bfloat16),
            neg_row.astype(jnp.bfloat16),
            jnp.zeros((q_rows, 32 - 3 * negs), jnp.bfloat16),
        ],
        axis=1,
    )
    cols_per = all_rows // blk_count
    packed = jnp.concatenate(
        [
            soft_grad.reshape(q_rows, blk_count, cols_per),
            jnp.broadcast_to(extra[:, None, :], (q_rows, blk_count, 32)),
        ],
        axis=2,
    ).reshape(q_rows, blk_count * (cols_per + 32))
    moved = lax.all_to_all(packed, "blk", split_axis=1, concat_axis=0, tiled=True)
    soft_cols = moved[:, :cols_per]
    all_hard = moved[:, cols_per:cols_per + negs]
    all_ids = (
        moved[:, cols_per + negs:cols_per + 2 * negs].astype(jnp.int32) * rows_shard
        + moved[:, cols_per + 2 * negs:cols_per + 3 * negs].astype(jnp.int32)
    )
    passage_grad = lax.dot_general(
        soft_cols, all_queries, (((0,), (0,)), ((), ())), preferred_element_type=jnp.float32
    )

    per_col = blk_count // owner_count
    piece_width = col_width // per_col
    shard = blk_index // per_col
    part = blk_index % per_col
    shard_iota = shard * rows_shard + jnp.arange(rows_shard, dtype=jnp.int32)
    shard_picks = all_ids[:, :, None] == shard_iota[None, None, :]
    shard_mix = jnp.sum(
        jnp.where(shard_picks, all_hard.astype(jnp.float32)[:, :, None], 0.0), axis=1
    )
    shard_hi, shard_lo = hi_lo(shard_mix)
    query_part = lax.dynamic_slice_in_dim(all_queries, part * piece_width, piece_width, axis=1)
    dims = (((0,), (0,)), ((), ()))
    piece = lax.dot_general(
        shard_hi, query_part, dims, preferred_element_type=jnp.float32
    ) + lax.dot_general(shard_lo, query_part, dims, preferred_element_type=jnp.float32)
    perm = []
    for b in range(blk_count):
        for c in range(owner_count):
            dest_b = c * per_col + b % per_col
            dest_c = b // per_col
            perm.append((b * owner_count + c, dest_b * owner_count + dest_c))
    table_grad = lax.ppermute(piece, ("blk", "corpus"), perm)
    return (loss_share, query_grad, passage_grad, table_grad)


def solution(mesh):
    placed = (
        P("blk", "corpus"),
        P("blk", "corpus"),
        P("corpus", None),
        P("blk", None),
        P("blk", None),
        P("blk"),
        P("blk"),
    )
    return jax.shard_map(
        per_device_body,
        mesh=mesh,
        in_specs=placed,
        out_specs=(
            P(("blk", "corpus")),
            P("blk", "corpus"),
            P("blk", "corpus"),
            P("corpus", "blk"),
        ),
        check_vma=False,
    )
```

```python
import jax
import jax.numpy as jnp
from jax import lax
from jax.sharding import PartitionSpec as P


def hi_lo(mixing):
    upper = mixing.astype(jnp.bfloat16)
    lower = (mixing - upper.astype(jnp.float32)).astype(jnp.bfloat16)
    return upper, lower


def gather_blocks(own, received, index, count):
    candidates = [own] + list(received)
    blocks = []
    for place in range(count):
        shift = (index - place) % count
        block = candidates[0]
        for k in range(1, count):
            block = jnp.where(shift == k, candidates[k], block)
        blocks.append(block)
    return jnp.concatenate(blocks, axis=0)


def per_device_body(queries, passages, table, neg_owner, neg_row, positive, loss_weight):
    q_rows, col_width = queries.shape
    owner_count = lax.axis_size("corpus")
    blk_count = lax.axis_size("blk")
    factor = (col_width * owner_count) ** (-0.5)
    rows_shard = table.shape[0]
    table_rows = owner_count * rows_shard
    owner_index = lax.axis_index("corpus")
    blk_index = lax.axis_index("blk")

    slice_of = lambda k: lax.dynamic_slice_in_dim(
        table, ((owner_index + k) % owner_count) * col_width, col_width, axis=1
    )
    received = []
    for k in range(1, owner_count):
        shift = [(j, (j + k) % owner_count) for j in range(owner_count)]
        received.append(lax.ppermute(slice_of(k), "corpus", shift))
    table_cols = gather_blocks(slice_of(0), received, owner_index, owner_count)
    all_passages = lax.all_gather(passages, "blk", axis=0, tiled=True)
    all_queries = lax.all_gather(queries, "blk", axis=0, tiled=True)
    ids = neg_owner * rows_shard + neg_row
    all_rows = all_passages.shape[0]

    logits = lax.dot_general(
        queries, all_passages, (((1,), (1,)), ((), ())), preferred_element_type=jnp.float32
    )
    table_scores = lax.dot_general(
        queries, table_cols, (((1,), (1,)), ((), ())), preferred_element_type=jnp.float32
    )
    row_iota = jnp.arange(table_rows, dtype=jnp.int32)
    picks = ids[:, :, None] == row_iota[None, None, :]
    hard_logits = jnp.sum(jnp.where(picks, table_scores[:, None, :], 0.0), axis=2)
    negs = ids.shape[1]
    pad = jnp.zeros((q_rows, 128 - negs), jnp.float32)
    partial = jnp.concatenate([logits, hard_logits, pad], axis=1)
    share = q_rows // owner_count
    chunk_of = lambda k: lax.dynamic_slice_in_dim(
        partial, ((owner_index + k) % owner_count) * share, share, axis=0
    )
    summed = chunk_of(0)
    for k in range(1, owner_count):
        shift = [(j, (j + k) % owner_count) for j in range(owner_count)]
        summed = summed + lax.ppermute(chunk_of(k), "corpus", shift)
    logits = summed[:, :all_rows] * factor
    hard_logits = summed[:, all_rows:all_rows + negs] * factor
    my_positive = lax.dynamic_slice_in_dim(positive, owner_index * share, share)
    my_weight = lax.dynamic_slice_in_dim(loss_weight, owner_index * share, share)
    row_top = jnp.maximum(jnp.max(logits, axis=1), jnp.max(hard_logits, axis=1))
    log_total = row_top + jnp.log(
        jnp.sum(jnp.exp(logits - row_top[:, None]), axis=1)
        + jnp.sum(jnp.exp(hard_logits - row_top[:, None]), axis=1)
    )
    one_hot = my_positive[:, None] == jnp.arange(all_rows, dtype=jnp.int32)[None, :]
    loss_share = log_total - jnp.sum(jnp.where(one_hot, logits, 0.0), axis=1)
    weighting = (my_weight * factor)[:, None]
    soft_part = (
        weighting * (jnp.exp(logits - log_total[:, None]) - one_hot.astype(jnp.float32))
    ).astype(jnp.bfloat16)
    hard_part = (weighting * jnp.exp(hard_logits - log_total[:, None])).astype(jnp.bfloat16)
    grads_part = jnp.concatenate(
        [soft_part, hard_part, jnp.zeros((share, 128 - negs), jnp.bfloat16)], axis=1
    )
    received = []
    for k in range(1, owner_count):
        shift = [(j, (j + k) % owner_count) for j in range(owner_count)]
        received.append(lax.ppermute(grads_part, "corpus", shift))
    grads = gather_blocks(grads_part, received, owner_index, owner_count)
    soft_grad = grads[:, :all_rows]
    hard_grad = grads[:, all_rows:all_rows + negs]

    mixing = jnp.sum(jnp.where(picks, hard_grad.astype(jnp.float32)[:, :, None], 0.0), axis=1)
    mix_hi, mix_lo = hi_lo(mixing)
    left = jnp.concatenate([soft_grad, mix_hi, mix_lo], axis=1)
    right = jnp.concatenate([all_passages, table_cols, table_cols], axis=0)
    query_grad = jnp.dot(left, right, preferred_element_type=jnp.float32)

    extra = jnp.concatenate(
        [
            hard_grad,
            neg_owner.astype(jnp.bfloat16),
            neg_row.astype(jnp.bfloat16),
            jnp.zeros((q_rows, 32 - 3 * negs), jnp.bfloat16),
        ],
        axis=1,
    )
    cols_per = all_rows // blk_count
    packed = jnp.concatenate(
        [
            soft_grad.reshape(q_rows, blk_count, cols_per),
            jnp.broadcast_to(extra[:, None, :], (q_rows, blk_count, 32)),
        ],
        axis=2,
    ).reshape(q_rows, blk_count * (cols_per + 32))
    moved = lax.all_to_all(packed, "blk", split_axis=1, concat_axis=0, tiled=True)
    soft_cols = moved[:, :cols_per]
    all_hard = moved[:, cols_per:cols_per + negs]
    all_ids = (
        moved[:, cols_per + negs:cols_per + 2 * negs].astype(jnp.int32) * rows_shard
        + moved[:, cols_per + 2 * negs:cols_per + 3 * negs].astype(jnp.int32)
    )
    passage_grad = lax.dot_general(
        soft_cols, all_queries, (((0,), (0,)), ((), ())), preferred_element_type=jnp.float32
    )

    per_col = blk_count // owner_count
    piece_width = col_width // per_col
    shard = blk_index // per_col
    part = blk_index % per_col
    shard_iota = shard * rows_shard + jnp.arange(rows_shard, dtype=jnp.int32)
    shard_picks = all_ids[:, :, None] == shard_iota[None, None, :]
    shard_mix = jnp.sum(
        jnp.where(shard_picks, all_hard.astype(jnp.float32)[:, :, None], 0.0), axis=1
    )
    shard_hi, shard_lo = hi_lo(shard_mix)
    query_part = lax.dynamic_slice_in_dim(all_queries, part * piece_width, piece_width, axis=1)
    dims = (((0,), (0,)), ((), ()))
    piece = lax.dot_general(
        shard_hi, query_part, dims, preferred_element_type=jnp.float32
    ) + lax.dot_general(shard_lo, query_part, dims, preferred_element_type=jnp.float32)
    perm = []
    for b in range(blk_count):
        for c in range(owner_count):
            dest_b = c * per_col + b % per_col
            dest_c = b // per_col
            perm.append((b * owner_count + c, dest_b * owner_count + dest_c))
    table_grad = lax.ppermute(piece, ("blk", "corpus"), perm)
    return (loss_share, query_grad, passage_grad, table_grad)


def solution(mesh):
    placed = (
        P("blk", "corpus"),
        P("blk", "corpus"),
        P("corpus", None),
        P("blk", None),
        P("blk", None),
        P("blk"),
        P("blk"),
    )
    return jax.shard_map(
        per_device_body,
        mesh=mesh,
        in_specs=placed,
        out_specs=(
            P(("blk", "corpus")),
            P("blk", "corpus"),
            P("blk", "corpus"),
            P("corpus", "blk"),
        ),
        check_vma=False,
    )
```

```python
import jax
import jax.numpy as jnp
from jax import lax
from jax.sharding import PartitionSpec as P


def hi_lo(mixing):
    upper = mixing.astype(jnp.bfloat16)
    lower = (mixing - upper.astype(jnp.float32)).astype(jnp.bfloat16)
    return upper, lower


def gather_blocks(own, received, index, count):
    candidates = [own] + list(received)
    blocks = []
    for place in range(count):
        shift = (index - place) % count
        block = candidates[0]
        for k in range(1, count):
            block = jnp.where(shift == k, candidates[k], block)
        blocks.append(block)
    return jnp.concatenate(blocks, axis=0)


def per_device_body(queries, passages, table, neg_owner, neg_row, positive, loss_weight):
    q_rows, col_width = queries.shape
    owner_count = lax.axis_size("corpus")
    blk_count = lax.axis_size("blk")
    factor = (col_width * owner_count) ** (-0.5)
    rows_shard = table.shape[0]
    table_rows = owner_count * rows_shard
    owner_index = lax.axis_index("corpus")
    blk_index = lax.axis_index("blk")

    slice_of = lambda k: lax.dynamic_slice_in_dim(
        table, ((owner_index + k) % owner_count) * col_width, col_width, axis=1
    )
    received = []
    for k in range(1, owner_count):
        shift = [(j, (j + k) % owner_count) for j in range(owner_count)]
        received.append(lax.ppermute(slice_of(k), "corpus", shift))
    table_cols = gather_blocks(slice_of(0), received, owner_index, owner_count)
    all_passages = lax.all_gather(passages, "blk", axis=0, tiled=True)
    all_queries = lax.all_gather(queries, "blk", axis=0, tiled=True)
    ids = neg_owner * rows_shard + neg_row
    all_rows = all_passages.shape[0]

    logits = lax.dot_general(
        queries, all_passages, (((1,), (1,)), ((), ())), preferred_element_type=jnp.float32
    )
    table_scores = lax.dot_general(
        queries, table_cols, (((1,), (1,)), ((), ())), preferred_element_type=jnp.float32
    )
    row_iota = jnp.arange(table_rows, dtype=jnp.int32)
    picks = ids[:, :, None] == row_iota[None, None, :]
    hard_logits = jnp.sum(jnp.where(picks, table_scores[:, None, :], 0.0), axis=2)
    negs = ids.shape[1]
    pad = jnp.zeros((q_rows, 128 - negs), jnp.float32)
    partial = jnp.concatenate([logits, hard_logits, pad], axis=1)
    share = q_rows // owner_count
    chunk_of = lambda k: lax.dynamic_slice_in_dim(
        partial, ((owner_index + k) % owner_count) * share, share, axis=0
    )
    summed = chunk_of(0)
    for k in range(1, owner_count):
        shift = [(j, (j + k) % owner_count) for j in range(owner_count)]
        summed = summed + lax.ppermute(chunk_of(k), "corpus", shift)
    logits = summed[:, :all_rows] * factor
    hard_logits = summed[:, all_rows:all_rows + negs] * factor
    my_positive = lax.dynamic_slice_in_dim(positive, owner_index * share, share)
    my_weight = lax.dynamic_slice_in_dim(loss_weight, owner_index * share, share)
    row_top = jnp.maximum(jnp.max(logits, axis=1), jnp.max(hard_logits, axis=1))
    log_total = row_top + jnp.log(
        jnp.sum(jnp.exp(logits - row_top[:, None]), axis=1)
        + jnp.sum(jnp.exp(hard_logits - row_top[:, None]), axis=1)
    )
    one_hot = my_positive[:, None] == jnp.arange(all_rows, dtype=jnp.int32)[None, :]
    loss_share = log_total - jnp.sum(jnp.where(one_hot, logits, 0.0), axis=1)
    weighting = (my_weight * factor)[:, None]
    soft_part = (
        weighting * (jnp.exp(logits - log_total[:, None]) - one_hot.astype(jnp.float32))
    ).astype(jnp.bfloat16)
    hard_part = (weighting * jnp.exp(hard_logits - log_total[:, None])).astype(jnp.bfloat16)
    grads_part = jnp.concatenate(
        [soft_part, hard_part, jnp.zeros((share, 128 - negs), jnp.bfloat16)], axis=1
    )
    received = []
    for k in range(1, owner_count):
        shift = [(j, (j + k) % owner_count) for j in range(owner_count)]
        received.append(lax.ppermute(grads_part, "corpus", shift))
    grads = gather_blocks(grads_part, received, owner_index, owner_count)
    soft_grad = grads[:, :all_rows]
    hard_grad = grads[:, all_rows:all_rows + negs]

    mixing = jnp.sum(jnp.where(picks, hard_grad.astype(jnp.float32)[:, :, None], 0.0), axis=1)
    mix_hi, mix_lo = hi_lo(mixing)
    query_grad = (
        jnp.dot(soft_grad, all_passages, preferred_element_type=jnp.float32)
        + jnp.dot(mix_hi, table_cols, preferred_element_type=jnp.float32)
        + jnp.dot(mix_lo, table_cols, preferred_element_type=jnp.float32)
    )

    extra = jnp.concatenate(
        [
            hard_grad,
            neg_owner.astype(jnp.bfloat16),
            neg_row.astype(jnp.bfloat16),
            jnp.zeros((q_rows, 32 - 3 * negs), jnp.bfloat16),
        ],
        axis=1,
    )
    cols_per = all_rows // blk_count
    packed = jnp.concatenate(
        [
            soft_grad.reshape(q_rows, blk_count, cols_per),
            jnp.broadcast_to(extra[:, None, :], (q_rows, blk_count, 32)),
        ],
        axis=2,
    ).reshape(q_rows, blk_count * (cols_per + 32))
    moved = lax.all_to_all(packed, "blk", split_axis=1, concat_axis=0, tiled=True)
    soft_cols = moved[:, :cols_per]
    all_hard = moved[:, cols_per:cols_per + negs]
    all_ids = (
        moved[:, cols_per + negs:cols_per + 2 * negs].astype(jnp.int32) * rows_shard
        + moved[:, cols_per + 2 * negs:cols_per + 3 * negs].astype(jnp.int32)
    )
    passage_grad = lax.dot_general(
        soft_cols, all_queries, (((0,), (0,)), ((), ())), preferred_element_type=jnp.float32
    )

    per_col = blk_count // owner_count
    piece_width = col_width // per_col
    shard = blk_index // per_col
    part = blk_index % per_col
    shard_iota = shard * rows_shard + jnp.arange(rows_shard, dtype=jnp.int32)
    shard_picks = all_ids[:, :, None] == shard_iota[None, None, :]
    shard_mix = jnp.sum(
        jnp.where(shard_picks, all_hard.astype(jnp.float32)[:, :, None], 0.0), axis=1
    )
    shard_hi, shard_lo = hi_lo(shard_mix)
    query_part = lax.dynamic_slice_in_dim(all_queries, part * piece_width, piece_width, axis=1)
    dims = (((0,), (0,)), ((), ()))
    piece = lax.dot_general(
        shard_hi, query_part, dims, preferred_element_type=jnp.float32
    ) + lax.dot_general(shard_lo, query_part, dims, preferred_element_type=jnp.float32)
    perm = []
    for b in range(blk_count):
        for c in range(owner_count):
            dest_b = c * per_col + b % per_col
            dest_c = b // per_col
            perm.append((b * owner_count + c, dest_b * owner_count + dest_c))
    table_grad = lax.ppermute(piece, ("blk", "corpus"), perm)
    return (loss_share, query_grad, passage_grad, table_grad)


def solution(mesh):
    placed = (
        P("blk", "corpus"),
        P("blk", "corpus"),
        P("corpus", None),
        P("blk", None),
        P("blk", None),
        P("blk"),
        P("blk"),
    )
    return jax.shard_map(
        per_device_body,
        mesh=mesh,
        in_specs=placed,
        out_specs=(
            P(("blk", "corpus")),
            P("blk", "corpus"),
            P("blk", "corpus"),
            P("corpus", "blk"),
        ),
        check_vma=False,
    )
```

```python
import jax
import jax.numpy as jnp
from jax import lax
from jax.sharding import PartitionSpec as P


def hi_lo(mixing):
    upper = mixing.astype(jnp.bfloat16)
    lower = (mixing - upper.astype(jnp.float32)).astype(jnp.bfloat16)
    return upper, lower


def gather_blocks(own, received, index, count):
    candidates = [own] + list(received)
    blocks = []
    for place in range(count):
        shift = (index - place) % count
        block = candidates[0]
        for k in range(1, count):
            block = jnp.where(shift == k, candidates[k], block)
        blocks.append(block)
    return jnp.concatenate(blocks, axis=0)


def per_device_body(queries, passages, table, neg_owner, neg_row, positive, loss_weight):
    q_rows, col_width = queries.shape
    owner_count = lax.axis_size("corpus")
    blk_count = lax.axis_size("blk")
    factor = (col_width * owner_count) ** (-0.5)
    rows_shard = table.shape[0]
    table_rows = owner_count * rows_shard
    owner_index = lax.axis_index("corpus")
    blk_index = lax.axis_index("blk")

    slice_of = lambda k: lax.dynamic_slice_in_dim(
        table, ((owner_index + k) % owner_count) * col_width, col_width, axis=1
    )
    received = []
    for k in range(1, owner_count):
        shift = [(j, (j + k) % owner_count) for j in range(owner_count)]
        received.append(lax.ppermute(slice_of(k), "corpus", shift))
    table_cols = gather_blocks(slice_of(0), received, owner_index, owner_count)
    all_passages = lax.all_gather(passages, "blk", axis=0, tiled=True)
    all_queries = lax.all_gather(queries, "blk", axis=0, tiled=True)
    ids = neg_owner * rows_shard + neg_row
    all_rows = all_passages.shape[0]

    logits = lax.dot_general(
        queries, all_passages, (((1,), (1,)), ((), ())), preferred_element_type=jnp.float32
    )
    table_scores = lax.dot_general(
        queries, table_cols, (((1,), (1,)), ((), ())), preferred_element_type=jnp.float32
    )
    row_iota = jnp.arange(table_rows, dtype=jnp.int32)
    picks = ids[:, :, None] == row_iota[None, None, :]
    hard_logits = jnp.sum(jnp.where(picks, table_scores[:, None, :], 0.0), axis=2)
    negs = ids.shape[1]
    pad = jnp.zeros((q_rows, 128 - negs), jnp.float32)
    partial = jnp.concatenate([logits, hard_logits, pad], axis=1)
    share = q_rows // owner_count
    chunk_of = lambda k: lax.dynamic_slice_in_dim(
        partial, ((owner_index + k) % owner_count) * share, share, axis=0
    )
    summed = chunk_of(0)
    for k in range(1, owner_count):
        shift = [(j, (j + k) % owner_count) for j in range(owner_count)]
        summed = summed + lax.ppermute(chunk_of(k), "corpus", shift)
    logits = summed[:, :all_rows] * factor
    hard_logits = summed[:, all_rows:all_rows + negs] * factor
    my_positive = lax.dynamic_slice_in_dim(positive, owner_index * share, share)
    my_weight = lax.dynamic_slice_in_dim(loss_weight, owner_index * share, share)
    row_top = jnp.maximum(jnp.max(logits, axis=1), jnp.max(hard_logits, axis=1))
    log_total = row_top + jnp.log(
        jnp.sum(jnp.exp(logits - row_top[:, None]), axis=1)
        + jnp.sum(jnp.exp(hard_logits - row_top[:, None]), axis=1)
    )
    one_hot = my_positive[:, None] == jnp.arange(all_rows, dtype=jnp.int32)[None, :]
    loss_share = log_total - jnp.sum(jnp.where(one_hot, logits, 0.0), axis=1)
    weighting = (my_weight * factor)[:, None]
    soft_part = (
        weighting * (jnp.exp(logits - log_total[:, None]) - one_hot.astype(jnp.float32))
    ).astype(jnp.bfloat16)
    hard_part = (weighting * jnp.exp(hard_logits - log_total[:, None])).astype(jnp.bfloat16)
    grads_part = jnp.concatenate(
        [soft_part, hard_part, jnp.zeros((share, 128 - negs), jnp.bfloat16)], axis=1
    )
    received = []
    for k in range(1, owner_count):
        shift = [(j, (j + k) % owner_count) for j in range(owner_count)]
        received.append(lax.ppermute(grads_part, "corpus", shift))
    grads = gather_blocks(grads_part, received, owner_index, owner_count)
    soft_grad = grads[:, :all_rows]
    hard_grad = grads[:, all_rows:all_rows + negs]

    mixing = jnp.sum(jnp.where(picks, hard_grad.astype(jnp.float32)[:, :, None], 0.0), axis=1)
    mix_hi, mix_lo = hi_lo(mixing)
    query_grad = (
        jnp.dot(soft_grad, all_passages, preferred_element_type=jnp.float32)
        + jnp.dot(mix_hi, table_cols, preferred_element_type=jnp.float32)
        + jnp.dot(mix_lo, table_cols, preferred_element_type=jnp.float32)
    )

    extra = jnp.concatenate(
        [
            hard_grad,
            neg_owner.astype(jnp.bfloat16),
            neg_row.astype(jnp.bfloat16),
            jnp.zeros((q_rows, 32 - 3 * negs), jnp.bfloat16),
        ],
        axis=1,
    )
    cols_per = all_rows // blk_count
    packed = jnp.concatenate(
        [
            soft_grad.reshape(q_rows, blk_count, cols_per),
            jnp.broadcast_to(extra[:, None, :], (q_rows, blk_count, 32)),
        ],
        axis=2,
    ).reshape(q_rows, blk_count * (cols_per + 32))
    moved = lax.all_to_all(packed, "blk", split_axis=1, concat_axis=0, tiled=True)
    soft_cols = moved[:, :cols_per]
    all_hard = moved[:, cols_per:cols_per + negs]
    all_ids = (
        moved[:, cols_per + negs:cols_per + 2 * negs].astype(jnp.int32) * rows_shard
        + moved[:, cols_per + 2 * negs:cols_per + 3 * negs].astype(jnp.int32)
    )
    passage_grad = lax.dot_general(
        soft_cols, all_queries, (((0,), (0,)), ((), ())), preferred_element_type=jnp.float32
    )

    per_col = blk_count // owner_count
    half = blk_count // 2
    piece_width = col_width // per_col
    first = 2 * (blk_index % half)
    part = first // owner_count
    shard = first % owner_count
    pair_iota = shard * rows_shard + jnp.arange(2 * rows_shard, dtype=jnp.int32)
    pair_picks = all_ids[:, :, None] == pair_iota[None, None, :]
    pair_mix = jnp.sum(
        jnp.where(pair_picks, all_hard.astype(jnp.float32)[:, :, None], 0.0), axis=1
    )
    pair_hi, pair_lo = hi_lo(pair_mix)
    query_part = lax.dynamic_slice_in_dim(all_queries, part * piece_width, piece_width, axis=1)
    dims = (((0,), (0,)), ((), ()))
    pieces = lax.dot_general(
        pair_hi, query_part, dims, preferred_element_type=jnp.float32
    ) + lax.dot_general(pair_lo, query_part, dims, preferred_element_type=jnp.float32)
    perms = ([], [])
    for c in range(owner_count):
        side = (c * per_col) // half
        for r in range(half):
            b = side * half + r
            for j in range(2):
                q = 2 * r + j
                dest_b = c * per_col + q // owner_count
                dest_c = q % owner_count
                perms[j].append((b * owner_count + c, dest_b * owner_count + dest_c))
    table_grad = lax.ppermute(
        pieces[:rows_shard], ("blk", "corpus"), perms[0]
    ) + lax.ppermute(pieces[rows_shard:], ("blk", "corpus"), perms[1])
    return (loss_share, query_grad, passage_grad, table_grad)


def solution(mesh):
    placed = (
        P("blk", "corpus"),
        P("blk", "corpus"),
        P("corpus", None),
        P("blk", None),
        P("blk", None),
        P("blk"),
        P("blk"),
    )
    return jax.shard_map(
        per_device_body,
        mesh=mesh,
        in_specs=placed,
        out_specs=(
            P(("blk", "corpus")),
            P("blk", "corpus"),
            P("blk", "corpus"),
            P("corpus", "blk"),
        ),
        check_vma=False,
    )
```

```python
import jax
import jax.numpy as jnp
from jax import lax
from jax.sharding import PartitionSpec as P


def hi_lo(mixing):
    upper = mixing.astype(jnp.bfloat16)
    lower = (mixing - upper.astype(jnp.float32)).astype(jnp.bfloat16)
    return upper, lower


def gather_blocks(own, received, index, count):
    candidates = [own] + list(received)
    blocks = []
    for place in range(count):
        shift = (index - place) % count
        block = candidates[0]
        for k in range(1, count):
            block = jnp.where(shift == k, candidates[k], block)
        blocks.append(block)
    return jnp.concatenate(blocks, axis=0)


def per_device_body(queries, passages, table, neg_owner, neg_row, positive, loss_weight):
    q_rows, col_width = queries.shape
    owner_count = lax.axis_size("corpus")
    blk_count = lax.axis_size("blk")
    factor = (col_width * owner_count) ** (-0.5)
    rows_shard = table.shape[0]
    table_rows = owner_count * rows_shard
    owner_index = lax.axis_index("corpus")
    blk_index = lax.axis_index("blk")

    slice_of = lambda k: lax.dynamic_slice_in_dim(
        table, ((owner_index + k) % owner_count) * col_width, col_width, axis=1
    )
    received = []
    for k in range(1, owner_count):
        shift = [(j, (j + k) % owner_count) for j in range(owner_count)]
        received.append(lax.ppermute(slice_of(k), "corpus", shift))
    table_cols = gather_blocks(slice_of(0), received, owner_index, owner_count)
    all_passages = lax.all_gather(passages, "blk", axis=0, tiled=True)
    all_queries = lax.all_gather(queries, "blk", axis=0, tiled=True)
    ids = neg_owner * rows_shard + neg_row
    all_rows = all_passages.shape[0]

    logits = lax.dot_general(
        queries, all_passages, (((1,), (1,)), ((), ())), preferred_element_type=jnp.float32
    )
    table_scores = lax.dot_general(
        queries, table_cols, (((1,), (1,)), ((), ())), preferred_element_type=jnp.float32
    )
    row_iota = jnp.arange(table_rows, dtype=jnp.int32)
    picks = ids[:, :, None] == row_iota[None, None, :]
    hard_logits = jnp.sum(jnp.where(picks, table_scores[:, None, :], 0.0), axis=2)
    negs = ids.shape[1]
    pad = jnp.zeros((q_rows, 128 - negs), jnp.float32)
    partial = jnp.concatenate([logits, hard_logits, pad], axis=1)
    share = q_rows // owner_count
    chunk_of = lambda k: lax.dynamic_slice_in_dim(
        partial, ((owner_index + k) % owner_count) * share, share, axis=0
    )
    summed = chunk_of(0)
    for k in range(1, owner_count):
        shift = [(j, (j + k) % owner_count) for j in range(owner_count)]
        summed = summed + lax.ppermute(chunk_of(k), "corpus", shift)
    logits = summed[:, :all_rows] * factor
    hard_logits = summed[:, all_rows:all_rows + negs] * factor
    my_positive = lax.dynamic_slice_in_dim(positive, owner_index * share, share)
    my_weight = lax.dynamic_slice_in_dim(loss_weight, owner_index * share, share)
    row_top = jnp.maximum(jnp.max(logits, axis=1), jnp.max(hard_logits, axis=1))
    log_total = row_top + jnp.log(
        jnp.sum(jnp.exp(logits - row_top[:, None]), axis=1)
        + jnp.sum(jnp.exp(hard_logits - row_top[:, None]), axis=1)
    )
    one_hot = my_positive[:, None] == jnp.arange(all_rows, dtype=jnp.int32)[None, :]
    loss_share = log_total - jnp.sum(jnp.where(one_hot, logits, 0.0), axis=1)
    weighting = (my_weight * factor)[:, None]
    soft_part = (
        weighting * (jnp.exp(logits - log_total[:, None]) - one_hot.astype(jnp.float32))
    ).astype(jnp.bfloat16)
    hard_part = (weighting * jnp.exp(hard_logits - log_total[:, None])).astype(jnp.bfloat16)
    grads_part = jnp.concatenate(
        [soft_part, hard_part, jnp.zeros((share, 128 - negs), jnp.bfloat16)], axis=1
    )
    received = []
    for k in range(1, owner_count):
        shift = [(j, (j + k) % owner_count) for j in range(owner_count)]
        received.append(lax.ppermute(grads_part, "corpus", shift))
    grads = gather_blocks(grads_part, received, owner_index, owner_count)
    soft_grad = grads[:, :all_rows]
    hard_grad = grads[:, all_rows:all_rows + negs]

    mixing = jnp.sum(jnp.where(picks, hard_grad.astype(jnp.float32)[:, :, None], 0.0), axis=1)
    mix_hi, mix_lo = hi_lo(mixing)
    query_grad = (
        jnp.dot(soft_grad, all_passages, preferred_element_type=jnp.float32)
        + jnp.dot(mix_hi, table_cols, preferred_element_type=jnp.float32)
        + jnp.dot(mix_lo, table_cols, preferred_element_type=jnp.float32)
    )

    extra = jnp.concatenate(
        [
            hard_grad,
            neg_owner.astype(jnp.bfloat16),
            neg_row.astype(jnp.bfloat16),
            jnp.zeros((q_rows, 32 - 3 * negs), jnp.bfloat16),
        ],
        axis=1,
    )
    cols_per = all_rows // blk_count
    packed = jnp.concatenate(
        [
            soft_grad.reshape(q_rows, blk_count, cols_per),
            jnp.broadcast_to(extra[:, None, :], (q_rows, blk_count, 32)),
        ],
        axis=2,
    ).reshape(q_rows, blk_count * (cols_per + 32))
    moved = lax.all_to_all(packed, "blk", split_axis=1, concat_axis=0, tiled=True)
    soft_cols = moved[:, :cols_per]
    all_hard = moved[:, cols_per:cols_per + negs]
    all_ids = (
        moved[:, cols_per + negs:cols_per + 2 * negs].astype(jnp.int32) * rows_shard
        + moved[:, cols_per + 2 * negs:cols_per + 3 * negs].astype(jnp.int32)
    )
    passage_grad = lax.dot_general(
        soft_cols, all_queries, (((0,), (0,)), ((), ())), preferred_element_type=jnp.float32
    )

    per_col = blk_count // owner_count
    piece_width = col_width // per_col
    part = blk_index % per_col
    holder = blk_index // per_col
    all_picks = all_ids[:, :, None] == row_iota[None, None, :]
    all_mix = jnp.sum(jnp.where(all_picks, all_hard.astype(jnp.float32)[:, :, None], 0.0), axis=1)
    all_hi, all_lo = hi_lo(all_mix)
    query_part = lax.dynamic_slice_in_dim(all_queries, part * piece_width, piece_width, axis=1)
    dims = (((0,), (0,)), ((), ()))
    pieces = lax.dot_general(
        all_hi, query_part, dims, preferred_element_type=jnp.float32
    ) + lax.dot_general(all_lo, query_part, dims, preferred_element_type=jnp.float32)
    own = lax.dynamic_slice_in_dim(pieces, owner_index * rows_shard, rows_shard, axis=0)
    table_grad = jnp.where(owner_index == holder, own, 0.0)
    for k in range(1, owner_count):
        pairs = [
            (b * owner_count + b // per_col, b * owner_count + (b // per_col + k) % owner_count)
            for b in range(blk_count)
        ]
        sent = lax.dynamic_slice_in_dim(
            pieces, ((owner_index + k) % owner_count) * rows_shard, rows_shard, axis=0
        )
        table_grad = table_grad + lax.ppermute(sent, ("blk", "corpus"), pairs)
    return (loss_share, query_grad, passage_grad, table_grad)


def solution(mesh):
    placed = (
        P("blk", "corpus"),
        P("blk", "corpus"),
        P("corpus", None),
        P("blk", None),
        P("blk", None),
        P("blk"),
        P("blk"),
    )
    return jax.shard_map(
        per_device_body,
        mesh=mesh,
        in_specs=placed,
        out_specs=(
            P(("blk", "corpus")),
            P("blk", "corpus"),
            P("blk", "corpus"),
            P("corpus", "blk"),
        ),
        check_vma=False,
    )
```

```python
import jax
import jax.numpy as jnp
from jax import lax
from jax.sharding import PartitionSpec as P


def hi_lo(mixing):
    upper = mixing.astype(jnp.bfloat16)
    lower = (mixing - upper.astype(jnp.float32)).astype(jnp.bfloat16)
    return upper, lower


def gather_blocks(own, received, index, count):
    candidates = [own] + list(received)
    blocks = []
    for place in range(count):
        shift = (index - place) % count
        block = candidates[0]
        for k in range(1, count):
            block = jnp.where(shift == k, candidates[k], block)
        blocks.append(block)
    return jnp.concatenate(blocks, axis=0)


def per_device_body(queries, passages, table, neg_owner, neg_row, positive, loss_weight):
    q_rows, col_width = queries.shape
    owner_count = lax.axis_size("corpus")
    blk_count = lax.axis_size("blk")
    factor = (col_width * owner_count) ** (-0.5)
    rows_shard = table.shape[0]
    table_rows = owner_count * rows_shard
    owner_index = lax.axis_index("corpus")
    blk_index = lax.axis_index("blk")

    slice_of = lambda k: lax.dynamic_slice_in_dim(
        table, ((owner_index + k) % owner_count) * col_width, col_width, axis=1
    )
    received = []
    for k in range(1, owner_count):
        shift = [(j, (j + k) % owner_count) for j in range(owner_count)]
        received.append(lax.ppermute(slice_of(k), "corpus", shift))
    table_cols = gather_blocks(slice_of(0), received, owner_index, owner_count)
    received = []
    for k in range(1, blk_count):
        shift = [(j, (j + k) % blk_count) for j in range(blk_count)]
        received.append(lax.ppermute(passages, "blk", shift))
    all_passages = gather_blocks(passages, received, blk_index, blk_count)
    all_passages, later = lax.optimization_barrier((all_passages, queries))
    received = []
    for k in range(1, blk_count):
        shift = [(j, (j + k) % blk_count) for j in range(blk_count)]
        received.append(lax.ppermute(later, "blk", shift))
    all_queries = gather_blocks(later, received, blk_index, blk_count)
    ids = neg_owner * rows_shard + neg_row
    all_rows = all_passages.shape[0]

    logits = lax.dot_general(
        queries, all_passages, (((1,), (1,)), ((), ())), preferred_element_type=jnp.float32
    )
    table_scores = lax.dot_general(
        queries, table_cols, (((1,), (1,)), ((), ())), preferred_element_type=jnp.float32
    )
    row_iota = jnp.arange(table_rows, dtype=jnp.int32)
    picks = ids[:, :, None] == row_iota[None, None, :]
    hard_logits = jnp.sum(jnp.where(picks, table_scores[:, None, :], 0.0), axis=2)
    negs = ids.shape[1]
    pad = jnp.zeros((q_rows, 128 - negs), jnp.float32)
    partial = jnp.concatenate([logits, hard_logits, pad], axis=1)
    share = q_rows // owner_count
    chunk_of = lambda k: lax.dynamic_slice_in_dim(
        partial, ((owner_index + k) % owner_count) * share, share, axis=0
    )
    summed = chunk_of(0)
    for k in range(1, owner_count):
        shift = [(j, (j + k) % owner_count) for j in range(owner_count)]
        got = lax.ppermute(chunk_of(k), "corpus", shift)
        summed = summed + got
    logits = summed[:, :all_rows] * factor
    hard_logits = summed[:, all_rows:all_rows + negs] * factor
    my_positive = lax.dynamic_slice_in_dim(positive, owner_index * share, share)
    my_weight = lax.dynamic_slice_in_dim(loss_weight, owner_index * share, share)
    row_top = jnp.maximum(jnp.max(logits, axis=1), jnp.max(hard_logits, axis=1))
    log_total = row_top + jnp.log(
        jnp.sum(jnp.exp(logits - row_top[:, None]), axis=1)
        + jnp.sum(jnp.exp(hard_logits - row_top[:, None]), axis=1)
    )
    one_hot = my_positive[:, None] == jnp.arange(all_rows, dtype=jnp.int32)[None, :]
    loss_share = log_total - jnp.sum(jnp.where(one_hot, logits, 0.0), axis=1)
    weighting = (my_weight * factor)[:, None]
    soft_part = (
        weighting * (jnp.exp(logits - log_total[:, None]) - one_hot.astype(jnp.float32))
    ).astype(jnp.bfloat16)
    hard_part = (weighting * jnp.exp(hard_logits - log_total[:, None])).astype(jnp.bfloat16)
    grads_part = jnp.concatenate(
        [soft_part, hard_part, jnp.zeros((share, 128 - negs), jnp.bfloat16)], axis=1
    )
    received = []
    for k in range(1, owner_count):
        shift = [(j, (j + k) % owner_count) for j in range(owner_count)]
        received.append(lax.ppermute(grads_part, "corpus", shift))
    grads = gather_blocks(grads_part, received, owner_index, owner_count)
    soft_grad = grads[:, :all_rows]
    hard_grad = grads[:, all_rows:all_rows + negs]

    mixing = jnp.sum(jnp.where(picks, hard_grad.astype(jnp.float32)[:, :, None], 0.0), axis=1)
    mix_hi, mix_lo = hi_lo(mixing)
    query_grad = (
        jnp.dot(soft_grad, all_passages, preferred_element_type=jnp.float32)
        + jnp.dot(mix_hi, table_cols, preferred_element_type=jnp.float32)
        + jnp.dot(mix_lo, table_cols, preferred_element_type=jnp.float32)
    )

    extra = jnp.concatenate(
        [
            hard_grad,
            neg_owner.astype(jnp.bfloat16),
            neg_row.astype(jnp.bfloat16),
            jnp.zeros((q_rows, 32 - 3 * negs), jnp.bfloat16),
        ],
        axis=1,
    )
    cols_per = all_rows // blk_count
    packed = jnp.concatenate(
        [
            soft_grad.reshape(q_rows, blk_count, cols_per),
            jnp.broadcast_to(extra[:, None, :], (q_rows, blk_count, 32)),
        ],
        axis=2,
    ).reshape(q_rows, blk_count * (cols_per + 32))
    moved = lax.all_to_all(packed, "blk", split_axis=1, concat_axis=0, tiled=True)
    soft_cols = moved[:, :cols_per]
    all_hard = moved[:, cols_per:cols_per + negs]
    all_ids = (
        moved[:, cols_per + negs:cols_per + 2 * negs].astype(jnp.int32) * rows_shard
        + moved[:, cols_per + 2 * negs:cols_per + 3 * negs].astype(jnp.int32)
    )
    passage_grad = lax.dot_general(
        soft_cols, all_queries, (((0,), (0,)), ((), ())), preferred_element_type=jnp.float32
    )

    per_col = blk_count // owner_count
    piece_width = col_width // per_col
    part = blk_index % per_col
    holder = blk_index // per_col
    all_picks = all_ids[:, :, None] == row_iota[None, None, :]
    all_mix = jnp.sum(jnp.where(all_picks, all_hard.astype(jnp.float32)[:, :, None], 0.0), axis=1)
    all_hi, all_lo = hi_lo(all_mix)
    query_part = lax.dynamic_slice_in_dim(all_queries, part * piece_width, piece_width, axis=1)
    dims = (((0,), (0,)), ((), ()))
    pieces = lax.dot_general(
        all_hi, query_part, dims, preferred_element_type=jnp.float32
    ) + lax.dot_general(all_lo, query_part, dims, preferred_element_type=jnp.float32)
    own = lax.dynamic_slice_in_dim(pieces, owner_index * rows_shard, rows_shard, axis=0)
    table_grad = jnp.where(owner_index == holder, own, 0.0)
    for k in range(1, owner_count):
        pairs = [
            (b * owner_count + b // per_col, b * owner_count + (b // per_col + k) % owner_count)
            for b in range(blk_count)
        ]
        sent = lax.dynamic_slice_in_dim(
            pieces, ((owner_index + k) % owner_count) * rows_shard, rows_shard, axis=0
        )
        table_grad = table_grad + lax.ppermute(sent, ("blk", "corpus"), pairs)
    return (loss_share, query_grad, passage_grad, table_grad)


def solution(mesh):
    placed = (
        P("blk", "corpus"),
        P("blk", "corpus"),
        P("corpus", None),
        P("blk", None),
        P("blk", None),
        P("blk"),
        P("blk"),
    )
    return jax.shard_map(
        per_device_body,
        mesh=mesh,
        in_specs=placed,
        out_specs=(
            P(("blk", "corpus")),
            P("blk", "corpus"),
            P("blk", "corpus"),
            P("corpus", "blk"),
        ),
        check_vma=False,
    )
```

```python
import jax
import jax.numpy as jnp
from jax import lax
from jax.sharding import PartitionSpec as P


def hi_lo(mixing):
    upper = mixing.astype(jnp.bfloat16)
    lower = (mixing - upper.astype(jnp.float32)).astype(jnp.bfloat16)
    return upper, lower


def gather_blocks(own, received, index, count):
    candidates = [own] + list(received)
    blocks = []
    for place in range(count):
        shift = (index - place) % count
        block = candidates[0]
        for k in range(1, count):
            block = jnp.where(shift == k, candidates[k], block)
        blocks.append(block)
    return jnp.concatenate(blocks, axis=0)


def per_device_body(queries, passages, table, neg_owner, neg_row, positive, loss_weight):
    q_rows, col_width = queries.shape
    owner_count = lax.axis_size("corpus")
    blk_count = lax.axis_size("blk")
    factor = (col_width * owner_count) ** (-0.5)
    rows_shard = table.shape[0]
    table_rows = owner_count * rows_shard
    owner_index = lax.axis_index("corpus")
    blk_index = lax.axis_index("blk")

    slice_of = lambda k: lax.dynamic_slice_in_dim(
        table, ((owner_index + k) % owner_count) * col_width, col_width, axis=1
    )
    received = []
    for k in range(1, owner_count):
        shift = [(j, (j + k) % owner_count) for j in range(owner_count)]
        received.append(lax.ppermute(slice_of(k), "corpus", shift))
    table_cols = jnp.concatenate([slice_of(0)] + received, axis=0)
    received = []
    for k in range(1, blk_count):
        shift = [(j, (j + k) % blk_count) for j in range(blk_count)]
        received.append(lax.ppermute(passages, "blk", shift))
    all_passages = jnp.concatenate([passages] + received, axis=0)
    all_passages, later = lax.optimization_barrier((all_passages, queries))
    received = []
    for k in range(1, blk_count):
        shift = [(j, (j + k) % blk_count) for j in range(blk_count)]
        received.append(lax.ppermute(later, "blk", shift))
    all_queries = jnp.concatenate([later] + received, axis=0)
    ids = neg_owner * rows_shard + neg_row
    all_rows = all_passages.shape[0]

    logits = lax.dot_general(
        queries, all_passages, (((1,), (1,)), ((), ())), preferred_element_type=jnp.float32
    )
    table_scores = lax.dot_general(
        queries, table_cols, (((1,), (1,)), ((), ())), preferred_element_type=jnp.float32
    )
    row_iota = jnp.arange(table_rows, dtype=jnp.int32)
    local_ids = ((owner_index - neg_owner) % owner_count) * rows_shard + neg_row
    picks = local_ids[:, :, None] == row_iota[None, None, :]
    hard_logits = jnp.sum(jnp.where(picks, table_scores[:, None, :], 0.0), axis=2)
    negs = ids.shape[1]
    pad = jnp.zeros((q_rows, 128 - negs), jnp.float32)
    partial = jnp.concatenate([logits, hard_logits, pad], axis=1)
    share = q_rows // owner_count
    chunk_of = lambda k: lax.dynamic_slice_in_dim(
        partial, ((owner_index + k) % owner_count) * share, share, axis=0
    )
    summed = chunk_of(0)
    for k in range(1, owner_count):
        shift = [(j, (j + k) % owner_count) for j in range(owner_count)]
        got = lax.ppermute(chunk_of(k), "corpus", shift)
        summed = summed + got
    logits = summed[:, :all_rows] * factor
    hard_logits = summed[:, all_rows:all_rows + negs] * factor
    my_positive = lax.dynamic_slice_in_dim(positive, owner_index * share, share)
    block_rows = all_rows // blk_count
    my_positive = ((blk_index - my_positive // block_rows) % blk_count) * block_rows + (
        my_positive % block_rows
    )
    my_weight = lax.dynamic_slice_in_dim(loss_weight, owner_index * share, share)
    row_top = jnp.maximum(jnp.max(logits, axis=1), jnp.max(hard_logits, axis=1))
    log_total = row_top + jnp.log(
        jnp.sum(jnp.exp(logits - row_top[:, None]), axis=1)
        + jnp.sum(jnp.exp(hard_logits - row_top[:, None]), axis=1)
    )
    one_hot = my_positive[:, None] == jnp.arange(all_rows, dtype=jnp.int32)[None, :]
    loss_share = log_total - jnp.sum(jnp.where(one_hot, logits, 0.0), axis=1)
    weighting = (my_weight * factor)[:, None]
    soft_part = (
        weighting * (jnp.exp(logits - log_total[:, None]) - one_hot.astype(jnp.float32))
    ).astype(jnp.bfloat16)
    hard_part = (weighting * jnp.exp(hard_logits - log_total[:, None])).astype(jnp.bfloat16)
    grads_part = jnp.concatenate(
        [soft_part, hard_part, jnp.zeros((share, 128 - negs), jnp.bfloat16)], axis=1
    )
    received = []
    for k in range(1, owner_count):
        shift = [(j, (j + k) % owner_count) for j in range(owner_count)]
        received.append(lax.ppermute(grads_part, "corpus", shift))
    grads = gather_blocks(grads_part, received, owner_index, owner_count)
    soft_grad = grads[:, :all_rows]
    hard_grad = grads[:, all_rows:all_rows + negs]

    mixing = jnp.sum(jnp.where(picks, hard_grad.astype(jnp.float32)[:, :, None], 0.0), axis=1)
    mix_hi, mix_lo = hi_lo(mixing)
    query_grad = (
        jnp.dot(soft_grad, all_passages, preferred_element_type=jnp.float32)
        + jnp.dot(mix_hi, table_cols, preferred_element_type=jnp.float32)
        + jnp.dot(mix_lo, table_cols, preferred_element_type=jnp.float32)
    )

    extra = jnp.concatenate(
        [
            hard_grad,
            neg_owner.astype(jnp.bfloat16),
            neg_row.astype(jnp.bfloat16),
            jnp.zeros((q_rows, 32 - 3 * negs), jnp.bfloat16),
        ],
        axis=1,
    )
    cols_per = all_rows // blk_count
    packed = jnp.concatenate(
        [
            soft_grad.reshape(q_rows, blk_count, cols_per),
            jnp.broadcast_to(extra[:, None, :], (q_rows, blk_count, 32)),
        ],
        axis=2,
    )
    back = (blk_index - jnp.arange(blk_count, dtype=jnp.int32)) % blk_count
    packed = jnp.take(packed, back, axis=1).reshape(q_rows, blk_count * (cols_per + 32))
    moved = lax.all_to_all(packed, "blk", split_axis=1, concat_axis=0, tiled=True)
    moved = jnp.take(moved.reshape(blk_count, q_rows, cols_per + 32), back, axis=0).reshape(
        blk_count * q_rows, cols_per + 32
    )
    soft_cols = moved[:, :cols_per]
    all_hard = moved[:, cols_per:cols_per + negs]
    all_ids = (
        moved[:, cols_per + negs:cols_per + 2 * negs].astype(jnp.int32) * rows_shard
        + moved[:, cols_per + 2 * negs:cols_per + 3 * negs].astype(jnp.int32)
    )
    passage_grad = lax.dot_general(
        soft_cols, all_queries, (((0,), (0,)), ((), ())), preferred_element_type=jnp.float32
    )

    per_col = blk_count // owner_count
    piece_width = col_width // per_col
    part = blk_index % per_col
    holder = blk_index // per_col
    all_picks = all_ids[:, :, None] == row_iota[None, None, :]
    all_mix = jnp.sum(jnp.where(all_picks, all_hard.astype(jnp.float32)[:, :, None], 0.0), axis=1)
    all_hi, all_lo = hi_lo(all_mix)
    query_part = lax.dynamic_slice_in_dim(all_queries, part * piece_width, piece_width, axis=1)
    dims = (((0,), (0,)), ((), ()))
    pieces = lax.dot_general(
        all_hi, query_part, dims, preferred_element_type=jnp.float32
    ) + lax.dot_general(all_lo, query_part, dims, preferred_element_type=jnp.float32)
    own = lax.dynamic_slice_in_dim(pieces, owner_index * rows_shard, rows_shard, axis=0)
    table_grad = jnp.where(owner_index == holder, own, 0.0)
    for k in range(1, owner_count):
        pairs = [
            (b * owner_count + b // per_col, b * owner_count + (b // per_col + k) % owner_count)
            for b in range(blk_count)
        ]
        sent = lax.dynamic_slice_in_dim(
            pieces, ((owner_index + k) % owner_count) * rows_shard, rows_shard, axis=0
        )
        table_grad = table_grad + lax.ppermute(sent, ("blk", "corpus"), pairs)
    return (loss_share, query_grad, passage_grad, table_grad)


def solution(mesh):
    placed = (
        P("blk", "corpus"),
        P("blk", "corpus"),
        P("corpus", None),
        P("blk", None),
        P("blk", None),
        P("blk"),
        P("blk"),
    )
    return jax.shard_map(
        per_device_body,
        mesh=mesh,
        in_specs=placed,
        out_specs=(
            P(("blk", "corpus")),
            P("blk", "corpus"),
            P("blk", "corpus"),
            P("corpus", "blk"),
        ),
        check_vma=False,
    )
```

```python
import jax
import jax.numpy as jnp
from jax import lax
from jax.sharding import PartitionSpec as P


def hi_lo(mixing):
    upper = mixing.astype(jnp.bfloat16)
    lower = (mixing - upper.astype(jnp.float32)).astype(jnp.bfloat16)
    return upper, lower


def gather_blocks(own, received, index, count):
    candidates = [own] + list(received)
    blocks = []
    for place in range(count):
        shift = (index - place) % count
        block = candidates[0]
        for k in range(1, count):
            block = jnp.where(shift == k, candidates[k], block)
        blocks.append(block)
    return jnp.concatenate(blocks, axis=0)


def per_device_body(queries, passages, table, neg_owner, neg_row, positive, loss_weight):
    q_rows, col_width = queries.shape
    owner_count = lax.axis_size("corpus")
    blk_count = lax.axis_size("blk")
    factor = (col_width * owner_count) ** (-0.5)
    rows_shard = table.shape[0]
    table_rows = owner_count * rows_shard
    owner_index = lax.axis_index("corpus")
    blk_index = lax.axis_index("blk")

    slice_of = lambda k: lax.dynamic_slice_in_dim(
        table, ((owner_index + k) % owner_count) * col_width, col_width, axis=1
    )
    received = []
    for k in range(1, owner_count):
        shift = [(j, (j + k) % owner_count) for j in range(owner_count)]
        received.append(lax.ppermute(slice_of(k), "corpus", shift))
    table_cols = jnp.concatenate([slice_of(0)] + received, axis=0)
    received = []
    for k in range(1, blk_count):
        shift = [(j, (j + k) % blk_count) for j in range(blk_count)]
        received.append(lax.ppermute(passages, "blk", shift))
    passage_blocks = [passages] + received
    passage_blocks, later = lax.optimization_barrier((passage_blocks, queries))
    received = []
    for k in range(1, blk_count):
        shift = [(j, (j + k) % blk_count) for j in range(blk_count)]
        received.append(lax.ppermute(later, "blk", shift))
    query_blocks = [later] + received
    ids = neg_owner * rows_shard + neg_row
    all_rows = q_rows * blk_count
    block_rows = q_rows

    logits = jnp.concatenate(
        [
            lax.dot_general(
                queries, block, (((1,), (1,)), ((), ())), preferred_element_type=jnp.float32
            )
            for block in passage_blocks
        ],
        axis=1,
    )
    table_scores = lax.dot_general(
        queries, table_cols, (((1,), (1,)), ((), ())), preferred_element_type=jnp.float32
    )
    row_iota = jnp.arange(table_rows, dtype=jnp.int32)
    local_ids = ((owner_index - neg_owner) % owner_count) * rows_shard + neg_row
    picks = local_ids[:, :, None] == row_iota[None, None, :]
    hard_logits = jnp.sum(jnp.where(picks, table_scores[:, None, :], 0.0), axis=2)
    negs = ids.shape[1]
    pad = jnp.zeros((q_rows, 128 - negs), jnp.float32)
    partial = jnp.concatenate([logits, hard_logits, pad], axis=1)
    share = q_rows // owner_count
    chunk_of = lambda k: lax.dynamic_slice_in_dim(
        partial, ((owner_index + k) % owner_count) * share, share, axis=0
    )
    summed = chunk_of(0)
    for k in range(1, owner_count):
        shift = [(j, (j + k) % owner_count) for j in range(owner_count)]
        got = lax.ppermute(chunk_of(k), "corpus", shift)
        summed = summed + got
    logits = summed[:, :all_rows] * factor
    hard_logits = summed[:, all_rows:all_rows + negs] * factor
    my_positive = lax.dynamic_slice_in_dim(positive, owner_index * share, share)
    my_positive = ((blk_index - my_positive // block_rows) % blk_count) * block_rows + (
        my_positive % block_rows
    )
    my_weight = lax.dynamic_slice_in_dim(loss_weight, owner_index * share, share)
    row_top = jnp.maximum(jnp.max(logits, axis=1), jnp.max(hard_logits, axis=1))
    log_total = row_top + jnp.log(
        jnp.sum(jnp.exp(logits - row_top[:, None]), axis=1)
        + jnp.sum(jnp.exp(hard_logits - row_top[:, None]), axis=1)
    )
    one_hot = my_positive[:, None] == jnp.arange(all_rows, dtype=jnp.int32)[None, :]
    loss_share = log_total - jnp.sum(jnp.where(one_hot, logits, 0.0), axis=1)
    weighting = (my_weight * factor)[:, None]
    soft_part = (
        weighting * (jnp.exp(logits - log_total[:, None]) - one_hot.astype(jnp.float32))
    ).astype(jnp.bfloat16)
    hard_part = (weighting * jnp.exp(hard_logits - log_total[:, None])).astype(jnp.bfloat16)
    grads_part = jnp.concatenate(
        [soft_part, hard_part, jnp.zeros((share, 128 - negs), jnp.bfloat16)], axis=1
    )
    received = []
    for k in range(1, owner_count):
        shift = [(j, (j + k) % owner_count) for j in range(owner_count)]
        received.append(lax.ppermute(grads_part, "corpus", shift))
    grads = gather_blocks(grads_part, received, owner_index, owner_count)
    soft_grad = grads[:, :all_rows]
    hard_grad = grads[:, all_rows:all_rows + negs]

    mixing = jnp.sum(jnp.where(picks, hard_grad.astype(jnp.float32)[:, :, None], 0.0), axis=1)
    mix_hi, mix_lo = hi_lo(mixing)
    query_grad = (
        sum(
            jnp.dot(
                soft_grad[:, k * block_rows:(k + 1) * block_rows],
                block,
                preferred_element_type=jnp.float32,
            )
            for k, block in enumerate(passage_blocks)
        )
        + jnp.dot(mix_hi, table_cols, preferred_element_type=jnp.float32)
        + jnp.dot(mix_lo, table_cols, preferred_element_type=jnp.float32)
    )

    extra = jnp.concatenate(
        [
            hard_grad,
            neg_owner.astype(jnp.bfloat16),
            neg_row.astype(jnp.bfloat16),
            jnp.zeros((q_rows, 32 - 3 * negs), jnp.bfloat16),
        ],
        axis=1,
    )
    cols_per = all_rows // blk_count
    packed = jnp.concatenate(
        [
            soft_grad.reshape(q_rows, blk_count, cols_per),
            jnp.broadcast_to(extra[:, None, :], (q_rows, blk_count, 32)),
        ],
        axis=2,
    )
    back = (blk_index - jnp.arange(blk_count, dtype=jnp.int32)) % blk_count
    packed = jnp.take(packed, back, axis=1).reshape(q_rows, blk_count * (cols_per + 32))
    moved = lax.all_to_all(packed, "blk", split_axis=1, concat_axis=0, tiled=True)
    moved = jnp.take(moved.reshape(blk_count, q_rows, cols_per + 32), back, axis=0).reshape(
        blk_count * q_rows, cols_per + 32
    )
    soft_cols = moved[:, :cols_per]
    all_hard = moved[:, cols_per:cols_per + negs]
    all_ids = (
        moved[:, cols_per + negs:cols_per + 2 * negs].astype(jnp.int32) * rows_shard
        + moved[:, cols_per + 2 * negs:cols_per + 3 * negs].astype(jnp.int32)
    )
    dims = (((0,), (0,)), ((), ()))
    passage_grad = sum(
        lax.dot_general(
            soft_cols[k * q_rows:(k + 1) * q_rows], block, dims, preferred_element_type=jnp.float32
        )
        for k, block in enumerate(query_blocks)
    )

    per_col = blk_count // owner_count
    piece_width = col_width // per_col
    part = blk_index % per_col
    holder = blk_index // per_col
    all_picks = all_ids[:, :, None] == row_iota[None, None, :]
    all_mix = jnp.sum(jnp.where(all_picks, all_hard.astype(jnp.float32)[:, :, None], 0.0), axis=1)
    all_hi, all_lo = hi_lo(all_mix)
    pieces = 0.0
    for k, block in enumerate(query_blocks):
        query_part = lax.dynamic_slice_in_dim(block, part * piece_width, piece_width, axis=1)
        rows = slice(k * q_rows, (k + 1) * q_rows)
        pieces = pieces + lax.dot_general(
            all_hi[rows], query_part, dims, preferred_element_type=jnp.float32
        ) + lax.dot_general(all_lo[rows], query_part, dims, preferred_element_type=jnp.float32)
    own = lax.dynamic_slice_in_dim(pieces, owner_index * rows_shard, rows_shard, axis=0)
    table_grad = jnp.where(owner_index == holder, own, 0.0)
    for k in range(1, owner_count):
        pairs = [
            (b * owner_count + b // per_col, b * owner_count + (b // per_col + k) % owner_count)
            for b in range(blk_count)
        ]
        sent = lax.dynamic_slice_in_dim(
            pieces, ((owner_index + k) % owner_count) * rows_shard, rows_shard, axis=0
        )
        table_grad = table_grad + lax.ppermute(sent, ("blk", "corpus"), pairs)
    return (loss_share, query_grad, passage_grad, table_grad)


def solution(mesh):
    placed = (
        P("blk", "corpus"),
        P("blk", "corpus"),
        P("corpus", None),
        P("blk", None),
        P("blk", None),
        P("blk"),
        P("blk"),
    )
    return jax.shard_map(
        per_device_body,
        mesh=mesh,
        in_specs=placed,
        out_specs=(
            P(("blk", "corpus")),
            P("blk", "corpus"),
            P("blk", "corpus"),
            P("corpus", "blk"),
        ),
        check_vma=False,
    )
```

```python
import jax
import jax.numpy as jnp
from jax import lax
from jax.sharding import PartitionSpec as P


def hi_lo(mixing):
    upper = mixing.astype(jnp.bfloat16)
    lower = (mixing - upper.astype(jnp.float32)).astype(jnp.bfloat16)
    return upper, lower


def gather_blocks(own, received, index, count):
    candidates = [own] + list(received)
    blocks = []
    for place in range(count):
        shift = (index - place) % count
        block = candidates[0]
        for k in range(1, count):
            block = jnp.where(shift == k, candidates[k], block)
        blocks.append(block)
    return jnp.concatenate(blocks, axis=0)


def per_device_body(queries, passages, table, neg_owner, neg_row, positive, loss_weight):
    q_rows, col_width = queries.shape
    owner_count = lax.axis_size("corpus")
    blk_count = lax.axis_size("blk")
    factor = (col_width * owner_count) ** (-0.5)
    rows_shard = table.shape[0]
    table_rows = owner_count * rows_shard
    owner_index = lax.axis_index("corpus")
    blk_index = lax.axis_index("blk")

    slice_of = lambda k: lax.dynamic_slice_in_dim(
        table, ((owner_index + k) % owner_count) * col_width, col_width, axis=1
    )
    received = []
    for k in range(1, owner_count):
        shift = [(j, (j + k) % owner_count) for j in range(owner_count)]
        received.append(lax.ppermute(slice_of(k), "corpus", shift))
    table_cols = gather_blocks(slice_of(0), received, owner_index, owner_count)
    received = []
    for k in range(1, blk_count):
        shift = [(j, (j + k) % blk_count) for j in range(blk_count)]
        received.append(lax.ppermute(passages, "blk", shift))
    all_passages = gather_blocks(passages, received, blk_index, blk_count)
    all_passages, later = lax.optimization_barrier((all_passages, queries))
    received = []
    for k in range(1, blk_count):
        shift = [(j, (j + k) % blk_count) for j in range(blk_count)]
        received.append(lax.ppermute(later, "blk", shift))
    all_queries = gather_blocks(later, received, blk_index, blk_count)
    per_col = blk_count // owner_count
    piece_width = col_width // per_col
    part = blk_index % per_col
    cut = lambda block: lax.dynamic_slice_in_dim(block, part * piece_width, piece_width, axis=1)
    query_part = gather_blocks(cut(later), [cut(r) for r in received], blk_index, blk_count)
    ids = neg_owner * rows_shard + neg_row
    all_rows = all_passages.shape[0]

    logits = lax.dot_general(
        queries, all_passages, (((1,), (1,)), ((), ())), preferred_element_type=jnp.float32
    )
    table_scores = lax.dot_general(
        queries, table_cols, (((1,), (1,)), ((), ())), preferred_element_type=jnp.float32
    )
    row_iota = jnp.arange(table_rows, dtype=jnp.int32)
    picks = ids[:, :, None] == row_iota[None, None, :]
    hard_logits = jnp.sum(jnp.where(picks, table_scores[:, None, :], 0.0), axis=2)
    negs = ids.shape[1]
    pad = jnp.zeros((q_rows, 128 - negs), jnp.float32)
    partial = jnp.concatenate([logits, hard_logits, pad], axis=1)
    share = q_rows // owner_count
    chunk_of = lambda k: lax.dynamic_slice_in_dim(
        partial, ((owner_index + k) % owner_count) * share, share, axis=0
    )
    summed = chunk_of(0)
    for k in range(1, owner_count):
        shift = [(j, (j + k) % owner_count) for j in range(owner_count)]
        got = lax.ppermute(chunk_of(k), "corpus", shift)
        summed = summed + got
    logits = summed[:, :all_rows] * factor
    hard_logits = summed[:, all_rows:all_rows + negs] * factor
    my_positive = lax.dynamic_slice_in_dim(positive, owner_index * share, share)
    my_weight = lax.dynamic_slice_in_dim(loss_weight, owner_index * share, share)
    row_top = jnp.maximum(jnp.max(logits, axis=1), jnp.max(hard_logits, axis=1))
    log_total = row_top + jnp.log(
        jnp.sum(jnp.exp(logits - row_top[:, None]), axis=1)
        + jnp.sum(jnp.exp(hard_logits - row_top[:, None]), axis=1)
    )
    one_hot = my_positive[:, None] == jnp.arange(all_rows, dtype=jnp.int32)[None, :]
    loss_share = log_total - jnp.sum(jnp.where(one_hot, logits, 0.0), axis=1)
    weighting = (my_weight * factor)[:, None]
    soft_part = (
        weighting * (jnp.exp(logits - log_total[:, None]) - one_hot.astype(jnp.float32))
    ).astype(jnp.bfloat16)
    hard_part = (weighting * jnp.exp(hard_logits - log_total[:, None])).astype(jnp.bfloat16)
    grads_part = jnp.concatenate(
        [soft_part, hard_part, jnp.zeros((share, 128 - negs), jnp.bfloat16)], axis=1
    )
    received = []
    for k in range(1, owner_count):
        shift = [(j, (j + k) % owner_count) for j in range(owner_count)]
        received.append(lax.ppermute(grads_part, "corpus", shift))
    grads = gather_blocks(grads_part, received, owner_index, owner_count)
    soft_grad = grads[:, :all_rows]
    hard_grad = grads[:, all_rows:all_rows + negs]

    mixing = jnp.sum(jnp.where(picks, hard_grad.astype(jnp.float32)[:, :, None], 0.0), axis=1)
    mix_hi, mix_lo = hi_lo(mixing)
    query_grad = (
        jnp.dot(soft_grad, all_passages, preferred_element_type=jnp.float32)
        + jnp.dot(mix_hi, table_cols, preferred_element_type=jnp.float32)
        + jnp.dot(mix_lo, table_cols, preferred_element_type=jnp.float32)
    )

    extra = jnp.concatenate(
        [
            hard_grad,
            neg_owner.astype(jnp.bfloat16),
            neg_row.astype(jnp.bfloat16),
            jnp.zeros((q_rows, 32 - 3 * negs), jnp.bfloat16),
        ],
        axis=1,
    )
    cols_per = all_rows // blk_count
    packed = jnp.concatenate(
        [
            soft_grad.reshape(q_rows, blk_count, cols_per),
            jnp.broadcast_to(extra[:, None, :], (q_rows, blk_count, 32)),
        ],
        axis=2,
    ).reshape(q_rows, blk_count * (cols_per + 32))
    moved = lax.all_to_all(packed, "blk", split_axis=1, concat_axis=0, tiled=True)
    soft_cols = moved[:, :cols_per]
    all_hard = moved[:, cols_per:cols_per + negs]
    all_ids = (
        moved[:, cols_per + negs:cols_per + 2 * negs].astype(jnp.int32) * rows_shard
        + moved[:, cols_per + 2 * negs:cols_per + 3 * negs].astype(jnp.int32)
    )
    passage_grad = lax.dot_general(
        soft_cols, all_queries, (((0,), (0,)), ((), ())), preferred_element_type=jnp.float32
    )

    holder = blk_index // per_col
    all_picks = all_ids[:, :, None] == row_iota[None, None, :]
    all_mix = jnp.sum(jnp.where(all_picks, all_hard.astype(jnp.float32)[:, :, None], 0.0), axis=1)
    all_hi, all_lo = hi_lo(all_mix)
    dims = (((0,), (0,)), ((), ()))
    pieces = lax.dot_general(
        all_hi, query_part, dims, preferred_element_type=jnp.float32
    ) + lax.dot_general(all_lo, query_part, dims, preferred_element_type=jnp.float32)
    own = lax.dynamic_slice_in_dim(pieces, owner_index * rows_shard, rows_shard, axis=0)
    table_grad = jnp.where(owner_index == holder, own, 0.0)
    pieces = pieces.astype(jnp.bfloat16)
    for k in range(1, owner_count):
        pairs = [
            (b * owner_count + b // per_col, b * owner_count + (b // per_col + k) % owner_count)
            for b in range(blk_count)
        ]
        sent = lax.dynamic_slice_in_dim(
            pieces, ((owner_index + k) % owner_count) * rows_shard, rows_shard, axis=0
        )
        table_grad = table_grad + lax.ppermute(sent, ("blk", "corpus"), pairs).astype(jnp.float32)
    return (loss_share, query_grad, passage_grad, table_grad)


def solution(mesh):
    placed = (
        P("blk", "corpus"),
        P("blk", "corpus"),
        P("corpus", None),
        P("blk", None),
        P("blk", None),
        P("blk"),
        P("blk"),
    )
    return jax.shard_map(
        per_device_body,
        mesh=mesh,
        in_specs=placed,
        out_specs=(
            P(("blk", "corpus")),
            P("blk", "corpus"),
            P("blk", "corpus"),
            P("corpus", "blk"),
        ),
        check_vma=False,
    )
```

```python
import jax
import jax.numpy as jnp
from jax import lax
from jax.sharding import PartitionSpec as P


def hi_lo(mixing):
    upper = mixing.astype(jnp.bfloat16)
    lower = (mixing - upper.astype(jnp.float32)).astype(jnp.bfloat16)
    return upper, lower


def gather_blocks(own, received, index, count):
    candidates = [own] + list(received)
    blocks = []
    for place in range(count):
        shift = (index - place) % count
        block = candidates[0]
        for k in range(1, count):
            block = jnp.where(shift == k, candidates[k], block)
        blocks.append(block)
    return jnp.concatenate(blocks, axis=0)


def per_device_body(queries, passages, table, neg_owner, neg_row, positive, loss_weight):
    q_rows, col_width = queries.shape
    owner_count = lax.axis_size("corpus")
    blk_count = lax.axis_size("blk")
    factor = (col_width * owner_count) ** (-0.5)
    rows_shard = table.shape[0]
    table_rows = owner_count * rows_shard
    owner_index = lax.axis_index("corpus")
    blk_index = lax.axis_index("blk")

    slice_of = lambda k: lax.dynamic_slice_in_dim(
        table, ((owner_index + k) % owner_count) * col_width, col_width, axis=1
    )
    received = []
    for k in range(1, owner_count):
        shift = [(j, (j + k) % owner_count) for j in range(owner_count)]
        received.append(lax.ppermute(slice_of(k), "corpus", shift))
    table_cols = gather_blocks(slice_of(0), received, owner_index, owner_count)
    received = []
    for k in range(1, blk_count):
        shift = [(j, (j + k) % blk_count) for j in range(blk_count)]
        received.append(lax.ppermute(passages, "blk", shift))
    all_passages = gather_blocks(passages, received, blk_index, blk_count)
    all_passages, later = lax.optimization_barrier((all_passages, queries))
    received = []
    for k in range(1, blk_count):
        shift = [(j, (j + k) % blk_count) for j in range(blk_count)]
        received.append(lax.ppermute(later, "blk", shift))
    query_received = received
    per_col = blk_count // owner_count
    piece_width = col_width // per_col
    part = blk_index % per_col
    cut = lambda block: lax.dynamic_slice_in_dim(block, part * piece_width, piece_width, axis=1)
    ids = neg_owner * rows_shard + neg_row
    all_rows = all_passages.shape[0]

    logits = lax.dot_general(
        queries, all_passages, (((1,), (1,)), ((), ())), preferred_element_type=jnp.float32
    )
    table_scores = lax.dot_general(
        queries, table_cols, (((1,), (1,)), ((), ())), preferred_element_type=jnp.float32
    )
    row_iota = jnp.arange(table_rows, dtype=jnp.int32)
    picks = ids[:, :, None] == row_iota[None, None, :]
    hard_logits = jnp.sum(jnp.where(picks, table_scores[:, None, :], 0.0), axis=2)
    negs = ids.shape[1]
    pad = jnp.zeros((q_rows, 128 - negs), jnp.float32)
    partial = jnp.concatenate([logits, hard_logits, pad], axis=1)
    share = q_rows // owner_count
    chunk_of = lambda k: lax.dynamic_slice_in_dim(
        partial, ((owner_index + k) % owner_count) * share, share, axis=0
    )
    summed = chunk_of(0)
    for k in range(1, owner_count):
        shift = [(j, (j + k) % owner_count) for j in range(owner_count)]
        got = lax.ppermute(chunk_of(k), "corpus", shift)
        summed = summed + got
    logits = summed[:, :all_rows] * factor
    hard_logits = summed[:, all_rows:all_rows + negs] * factor
    my_positive = lax.dynamic_slice_in_dim(positive, owner_index * share, share)
    my_weight = lax.dynamic_slice_in_dim(loss_weight, owner_index * share, share)
    row_top = jnp.maximum(jnp.max(logits, axis=1), jnp.max(hard_logits, axis=1))
    log_total = row_top + jnp.log(
        jnp.sum(jnp.exp(logits - row_top[:, None]), axis=1)
        + jnp.sum(jnp.exp(hard_logits - row_top[:, None]), axis=1)
    )
    one_hot = my_positive[:, None] == jnp.arange(all_rows, dtype=jnp.int32)[None, :]
    loss_share = log_total - jnp.sum(jnp.where(one_hot, logits, 0.0), axis=1)
    weighting = (my_weight * factor)[:, None]
    soft_part = (
        weighting * (jnp.exp(logits - log_total[:, None]) - one_hot.astype(jnp.float32))
    ).astype(jnp.bfloat16)
    hard_part = (weighting * jnp.exp(hard_logits - log_total[:, None])).astype(jnp.bfloat16)
    grads_part = jnp.concatenate(
        [soft_part, hard_part, jnp.zeros((share, 128 - negs), jnp.bfloat16)], axis=1
    )
    received = []
    for k in range(1, owner_count):
        shift = [(j, (j + k) % owner_count) for j in range(owner_count)]
        received.append(lax.ppermute(grads_part, "corpus", shift))
    grads = gather_blocks(grads_part, received, owner_index, owner_count)
    soft_grad = grads[:, :all_rows]
    hard_grad = grads[:, all_rows:all_rows + negs]

    mixing = jnp.sum(jnp.where(picks, hard_grad.astype(jnp.float32)[:, :, None], 0.0), axis=1)
    mix_hi, mix_lo = hi_lo(mixing)
    query_grad = (
        jnp.dot(soft_grad, all_passages, preferred_element_type=jnp.float32)
        + jnp.dot(mix_hi, table_cols, preferred_element_type=jnp.float32)
        + jnp.dot(mix_lo, table_cols, preferred_element_type=jnp.float32)
    )

    extra = jnp.concatenate(
        [
            hard_grad,
            neg_owner.astype(jnp.bfloat16),
            neg_row.astype(jnp.bfloat16),
            jnp.zeros((q_rows, 32 - 3 * negs), jnp.bfloat16),
        ],
        axis=1,
    )
    cols_per = all_rows // blk_count
    packed = jnp.concatenate(
        [
            soft_grad.reshape(q_rows, blk_count, cols_per),
            jnp.broadcast_to(extra[:, None, :], (q_rows, blk_count, 32)),
        ],
        axis=2,
    ).reshape(q_rows, blk_count * (cols_per + 32))
    moved = lax.all_to_all(packed, "blk", split_axis=1, concat_axis=0, tiled=True)
    soft_cols = moved[:, :cols_per]
    all_hard = moved[:, cols_per:cols_per + negs]
    all_ids = (
        moved[:, cols_per + negs:cols_per + 2 * negs].astype(jnp.int32) * rows_shard
        + moved[:, cols_per + 2 * negs:cols_per + 3 * negs].astype(jnp.int32)
    )

    holder = blk_index // per_col
    all_picks = all_ids[:, :, None] == row_iota[None, None, :]
    all_mix = jnp.sum(jnp.where(all_picks, all_hard.astype(jnp.float32)[:, :, None], 0.0), axis=1)
    all_hi, all_lo = hi_lo(all_mix)
    all_hi, all_lo, part_own, part_received = lax.optimization_barrier(
        (all_hi, all_lo, later, query_received)
    )
    query_part = gather_blocks(
        cut(part_own), [cut(r) for r in part_received], blk_index, blk_count
    )
    dims = (((0,), (0,)), ((), ()))
    pieces = lax.dot_general(
        all_hi, query_part, dims, preferred_element_type=jnp.float32
    ) + lax.dot_general(all_lo, query_part, dims, preferred_element_type=jnp.float32)
    pieces, later, query_received = lax.optimization_barrier((pieces, later, query_received))
    all_queries = gather_blocks(later, query_received, blk_index, blk_count)
    passage_grad = lax.dot_general(
        soft_cols, all_queries, (((0,), (0,)), ((), ())), preferred_element_type=jnp.float32
    )
    own = lax.dynamic_slice_in_dim(pieces, owner_index * rows_shard, rows_shard, axis=0)
    table_grad = jnp.where(owner_index == holder, own, 0.0)
    pieces = pieces.astype(jnp.bfloat16)
    for k in range(1, owner_count):
        pairs = [
            (b * owner_count + b // per_col, b * owner_count + (b // per_col + k) % owner_count)
            for b in range(blk_count)
        ]
        sent = lax.dynamic_slice_in_dim(
            pieces, ((owner_index + k) % owner_count) * rows_shard, rows_shard, axis=0
        )
        table_grad = table_grad + lax.ppermute(sent, ("blk", "corpus"), pairs).astype(jnp.float32)
    return (loss_share, query_grad, passage_grad, table_grad)


def solution(mesh):
    placed = (
        P("blk", "corpus"),
        P("blk", "corpus"),
        P("corpus", None),
        P("blk", None),
        P("blk", None),
        P("blk"),
        P("blk"),
    )
    return jax.shard_map(
        per_device_body,
        mesh=mesh,
        in_specs=placed,
        out_specs=(
            P(("blk", "corpus")),
            P("blk", "corpus"),
            P("blk", "corpus"),
            P("corpus", "blk"),
        ),
        check_vma=False,
    )
```

```python
import jax
import jax.numpy as jnp
from jax import lax
from jax.sharding import PartitionSpec as P


def hi_lo(mixing):
    upper = mixing.astype(jnp.bfloat16)
    lower = (mixing - upper.astype(jnp.float32)).astype(jnp.bfloat16)
    return upper, lower


def gather_blocks(own, received, index, count):
    candidates = [own] + list(received)
    blocks = []
    for place in range(count):
        shift = (index - place) % count
        block = candidates[0]
        for k in range(1, count):
            block = jnp.where(shift == k, candidates[k], block)
        blocks.append(block)
    return jnp.concatenate(blocks, axis=0)


def per_device_body(queries, passages, table, neg_owner, neg_row, positive, loss_weight):
    q_rows, col_width = queries.shape
    owner_count = lax.axis_size("corpus")
    blk_count = lax.axis_size("blk")
    factor = (col_width * owner_count) ** (-0.5)
    rows_shard = table.shape[0]
    table_rows = owner_count * rows_shard
    owner_index = lax.axis_index("corpus")
    blk_index = lax.axis_index("blk")

    slice_of = lambda k: lax.dynamic_slice_in_dim(
        table, ((owner_index + k) % owner_count) * col_width, col_width, axis=1
    )
    received = []
    for k in range(1, owner_count):
        shift = [(j, (j + k) % owner_count) for j in range(owner_count)]
        received.append(lax.ppermute(slice_of(k), "corpus", shift))
    table_cols = gather_blocks(slice_of(0), received, owner_index, owner_count)
    received = []
    for k in range(1, blk_count):
        shift = [(j, (j + k) % blk_count) for j in range(blk_count)]
        received.append(lax.ppermute(passages, "blk", shift))
    all_passages = gather_blocks(passages, received, blk_index, blk_count)
    all_passages, later = lax.optimization_barrier((all_passages, queries))
    received = []
    for k in range(1, blk_count):
        shift = [(j, (j + k) % blk_count) for j in range(blk_count)]
        received.append(lax.ppermute(later, "blk", shift))
    query_received = received
    per_col = blk_count // owner_count
    piece_width = col_width // per_col
    part = blk_index % per_col
    cut = lambda block: lax.dynamic_slice_in_dim(block, part * piece_width, piece_width, axis=1)
    query_part = gather_blocks(cut(later), [cut(r) for r in received], blk_index, blk_count)
    ids = neg_owner * rows_shard + neg_row
    all_rows = all_passages.shape[0]

    logits = lax.dot_general(
        queries, all_passages, (((1,), (1,)), ((), ())), preferred_element_type=jnp.float32
    )
    table_scores = lax.dot_general(
        queries, table_cols, (((1,), (1,)), ((), ())), preferred_element_type=jnp.float32
    )
    row_iota = jnp.arange(table_rows, dtype=jnp.int32)
    picks = ids[:, :, None] == row_iota[None, None, :]
    hard_logits = jnp.sum(jnp.where(picks, table_scores[:, None, :], 0.0), axis=2)
    negs = ids.shape[1]
    pad = jnp.zeros((q_rows, 8 - negs), jnp.float32)
    partial = jnp.concatenate([logits, hard_logits, pad], axis=1)
    share = q_rows // owner_count
    chunk_of = lambda k: lax.dynamic_slice_in_dim(
        partial, ((owner_index + k) % owner_count) * share, share, axis=0
    )
    summed = chunk_of(0)
    for k in range(1, owner_count):
        shift = [(j, (j + k) % owner_count) for j in range(owner_count)]
        got = lax.ppermute(chunk_of(k), "corpus", shift)
        summed = summed + got
    logits = summed[:, :all_rows] * factor
    hard_logits = summed[:, all_rows:all_rows + negs] * factor
    my_positive = lax.dynamic_slice_in_dim(positive, owner_index * share, share)
    my_weight = lax.dynamic_slice_in_dim(loss_weight, owner_index * share, share)
    row_top = jnp.maximum(jnp.max(logits, axis=1), jnp.max(hard_logits, axis=1))
    log_total = row_top + jnp.log(
        jnp.sum(jnp.exp(logits - row_top[:, None]), axis=1)
        + jnp.sum(jnp.exp(hard_logits - row_top[:, None]), axis=1)
    )
    one_hot = my_positive[:, None] == jnp.arange(all_rows, dtype=jnp.int32)[None, :]
    loss_share = log_total - jnp.sum(jnp.where(one_hot, logits, 0.0), axis=1)
    weighting = (my_weight * factor)[:, None]
    soft_part = (
        weighting * (jnp.exp(logits - log_total[:, None]) - one_hot.astype(jnp.float32))
    ).astype(jnp.bfloat16)
    hard_part = (weighting * jnp.exp(hard_logits - log_total[:, None])).astype(jnp.bfloat16)
    grads_part = jnp.concatenate(
        [soft_part, hard_part, jnp.zeros((share, 8 - negs), jnp.bfloat16)], axis=1
    )
    received = []
    for k in range(1, owner_count):
        shift = [(j, (j + k) % owner_count) for j in range(owner_count)]
        received.append(lax.ppermute(grads_part, "corpus", shift))
    grads = gather_blocks(grads_part, received, owner_index, owner_count)
    soft_grad = grads[:, :all_rows]
    hard_grad = grads[:, all_rows:all_rows + negs]

    mixing = jnp.sum(jnp.where(picks, hard_grad.astype(jnp.float32)[:, :, None], 0.0), axis=1)
    mix_hi, mix_lo = hi_lo(mixing)
    query_grad = (
        jnp.dot(soft_grad, all_passages, preferred_element_type=jnp.float32)
        + jnp.dot(mix_hi, table_cols, preferred_element_type=jnp.float32)
        + jnp.dot(mix_lo, table_cols, preferred_element_type=jnp.float32)
    )

    extra = jnp.concatenate(
        [
            hard_grad,
            neg_owner.astype(jnp.bfloat16),
            neg_row.astype(jnp.bfloat16),
            jnp.zeros((q_rows, 32 - 3 * negs), jnp.bfloat16),
        ],
        axis=1,
    )
    cols_per = all_rows // blk_count
    packed = jnp.concatenate(
        [
            soft_grad.reshape(q_rows, blk_count, cols_per),
            jnp.broadcast_to(extra[:, None, :], (q_rows, blk_count, 32)),
        ],
        axis=2,
    ).reshape(q_rows, blk_count * (cols_per + 32))
    moved = lax.all_to_all(packed, "blk", split_axis=1, concat_axis=0, tiled=True)
    soft_cols = moved[:, :cols_per]
    all_hard = moved[:, cols_per:cols_per + negs]
    all_ids = (
        moved[:, cols_per + negs:cols_per + 2 * negs].astype(jnp.int32) * rows_shard
        + moved[:, cols_per + 2 * negs:cols_per + 3 * negs].astype(jnp.int32)
    )

    holder = blk_index // per_col
    all_picks = all_ids[:, :, None] == row_iota[None, None, :]
    all_mix = jnp.sum(jnp.where(all_picks, all_hard.astype(jnp.float32)[:, :, None], 0.0), axis=1)
    all_hi, all_lo = hi_lo(all_mix)
    dims = (((0,), (0,)), ((), ()))
    pieces = lax.dot_general(
        all_hi, query_part, dims, preferred_element_type=jnp.float32
    ) + lax.dot_general(all_lo, query_part, dims, preferred_element_type=jnp.float32)
    pieces, later, query_received = lax.optimization_barrier((pieces, later, query_received))
    all_queries = gather_blocks(later, query_received, blk_index, blk_count)
    passage_grad = lax.dot_general(
        soft_cols, all_queries, (((0,), (0,)), ((), ())), preferred_element_type=jnp.float32
    )
    own = lax.dynamic_slice_in_dim(pieces, owner_index * rows_shard, rows_shard, axis=0)
    table_grad = jnp.where(owner_index == holder, own, 0.0)
    pieces = pieces.astype(jnp.bfloat16)
    for k in range(1, owner_count):
        pairs = [
            (b * owner_count + b // per_col, b * owner_count + (b // per_col + k) % owner_count)
            for b in range(blk_count)
        ]
        sent = lax.dynamic_slice_in_dim(
            pieces, ((owner_index + k) % owner_count) * rows_shard, rows_shard, axis=0
        )
        table_grad = table_grad + lax.ppermute(sent, ("blk", "corpus"), pairs).astype(jnp.float32)
    return (loss_share, query_grad, passage_grad, table_grad)


def solution(mesh):
    placed = (
        P("blk", "corpus"),
        P("blk", "corpus"),
        P("corpus", None),
        P("blk", None),
        P("blk", None),
        P("blk"),
        P("blk"),
    )
    return jax.shard_map(
        per_device_body,
        mesh=mesh,
        in_specs=placed,
        out_specs=(
            P(("blk", "corpus")),
            P("blk", "corpus"),
            P("blk", "corpus"),
            P("corpus", "blk"),
        ),
        check_vma=False,
    )
```
